256 devices in a mesh: dp: 16 (over y_lo, x, core), tensor: 16 (over y_hi, z).
Axes of the slice: x: 4, y: 4 (y_hi: 2, y_lo: 2; y = y_hi * 2 + y_lo), z: 8, core: 2. Of those that a mesh axis runs over, the one named last changes fastest.
Arguments:
- tokens: bfloat16 [12288, 8192], P(('dp', 'tensor')), may hold values from -6 to 6
- q_weight: bfloat16 [8192, 8192], P(None, 'tensor'), may hold values from -0.0625 to 0.0625
- pool_down: bfloat16 [128, 64, 8192], P('dp', None, 'tensor'), may hold values from -0.0625 to 0.0625
- pool_up: bfloat16 [128, 64, 8192], P('dp', None, 'tensor'), may hold values from -0.75 to 0.75
- block_units: int32 [16, 8], replicated, may hold values from 1 to 24, 48 in all within a row
- adapter_ids: int32 [16, 8], replicated, may hold values from 0 to 127, as said below
- location: int32 [128], replicated, may hold values from 0 to 127, as said below
Outputs:
- queries: bfloat16 [12288, 8192], P('dp', 'tensor')
The draws below stay inside these ranges and needn't reach their ends.
Inputs may be any that keep to these rules, and one draw needn't show every extreme that they name: `adapter_ids`: the 8 adapters of one group lie in pool rows of 8 different dp shards (row location[a] lies on shard location[a] // 8). A permutation: adapter a is held in pool row location[a]. `block_units`: each group's blocks sum to 48; the largest is exactly 24.
All inputs are finite; a program needn't handle non-finite values.
Results may differ from the reference program's by a relative error of at most 0.0029.
Values may be sent and summed in bfloat16 or wider, within the bound.
No kernel may reach another device: no remote copies, remote signals or barrier semaphores. Data moves between devices by JAX's collectives and lax.ppermute only.
A program may use at most 128 MiB of HBM per device.

```python
import math
import jax
import jax.numpy as jnp
import numpy as np
from jax import lax

D = 8192
QOUT = 8192
R = 64
POOL_DEV = 8
GROUPS = 16
GROUP = 768
TOKENS = 12288
POOL = 128
UNITS = 48
TEN = 8
MOST_UNITS = 24


def draw_pool_plan(key):
    base_key = jax.random.fold_in(key, 4242)
    key_location, key_shard, key_row = jax.random.split(base_key, 3)
    location = jax.random.permutation(key_location, POOL).astype(jnp.int32)
    holder = jnp.argsort(location, stable=True).astype(jnp.int32)
    shard_keys = jax.random.split(key_shard, GROUPS)
    shard_pick = jax.vmap(lambda single_key: jax.random.permutation(single_key, GROUPS)[:TEN])(shard_keys)
    row_pick = jax.random.randint(key_row, (GROUPS, TEN), 0, POOL_DEV)
    selected_slot = holder[(shard_pick * POOL_DEV + row_pick).astype(jnp.int32)]
    return (location, selected_slot.astype(jnp.int32))


def draw_location(key, part):
    return draw_pool_plan(key)[0]


def draw_adapter_ids(key, part):
    return draw_pool_plan(key)[1]


def steps_of(stream_key, extent, cuts, least, high):
    def one(dim, shards_of):
        draws = jax.random.uniform(jax.random.fold_in(jax.random.fold_in(stream_key, 6), dim), (shards_of,), jnp.float32, least / len(cuts), high / len(cuts))
        return jnp.repeat(jnp.exp(draws), extent[dim] // shards_of).reshape((-1,) + (1,) * (len(extent) - dim - 1))

    gain = one(*cuts[0])
    for cut in cuts[1:]:
        gain = gain * one(*cut)
    return gain


def length_profile(amount, total, bound, slope):
    portions = [(1 << 20) // math.isqrt(rank ** slope) + 1 for rank in range(2, amount + 1)]
    rest, counts = total - bound - (amount - 1), [1] * (amount - 1)
    while rest > 0:
        free = [i for i in range(amount - 1) if counts[i] < bound]
        mass, remaining = sum([portions[i] for i in free]), rest
        for i in free:
            addition = min(bound - counts[i], max(1, remaining * portions[i] // mass), rest)
            counts[i] = counts[i] + addition
            rest = rest - addition
    return np.array([bound] + counts)


def uneven_parts(key, number_of, total, limit, skew):
    if number_of == 2:
        one = jax.random.randint(key, (), max(1, total - limit), min(limit, total - 1) + 1)
        return jnp.stack([one, total - one])
    sizes = jnp.asarray(length_profile(number_of, total, limit, skew), jnp.int32)
    couples = (number_of - 1) // 2
    source_of, sink = sizes[1:1 + 2 * couples:2], sizes[2:2 + 2 * couples:2]
    slack = jnp.minimum(source_of - 1, limit - sink)
    shifted = jax.random.randint(jax.random.fold_in(key, 1), (couples,), 0, 1 << 20) % (slack + 1)
    sizes = sizes.at[1:1 + 2 * couples:2].set(source_of - shifted).at[2:2 + 2 * couples:2].set(sink + shifted)
    return sizes[jax.random.permutation(jax.random.fold_in(key, 2), number_of)]


def gaussian(stream_key, extent, deviation, reach, shards=(), held_as=jnp.bfloat16):
    gain = steps_of(stream_key, extent, shards, -0.22, 0.18) if shards else 1.0
    drawn = jax.random.normal(stream_key, extent, jnp.float32) * deviation * gain
    return jnp.minimum(jnp.maximum(drawn, -reach), reach).astype(held_as)


def setup_inputs(seed: int = 0) -> dict:
    arg_keys = jax.random.split(jax.random.key(seed), 8)
    return {
        "tokens": gaussian(arg_keys[0], (TOKENS, D), 1.0, 6.0, ((0, 256),)),
        "q_weight": gaussian(arg_keys[1], (D, QOUT), D ** -0.5, 0.0625, ((1, 16),)),
        "pool_down": gaussian(arg_keys[2], (POOL, R, D), D ** -0.5, 0.0625, ((0, 16), (2, 16))),
        "pool_up": gaussian(arg_keys[3], (POOL, R, QOUT), R ** -0.5, 0.75, ((0, 16), (2, 16))),
        "block_units": jax.vmap(lambda own: uneven_parts(own, TEN, UNITS, MOST_UNITS, 2))(jax.random.split(arg_keys[4], GROUPS)).reshape((GROUPS, TEN)).astype(jnp.int32),
        "adapter_ids": draw_adapter_ids(jax.random.fold_in(arg_keys[7], 71), 0),
        "location": draw_location(jax.random.fold_in(arg_keys[7], 71), 0),
    }


adapter_scale = 0.5


def tenant_mask(pool_unit_row, group_rows, tenants):
    block_ends = 16 * jnp.cumsum(pool_unit_row)
    positions = jnp.arange(group_rows, dtype=jnp.int32)
    tenant_index = jnp.sum((positions[:, None] >= block_ends[None, :]).astype(jnp.int32), axis=1)
    return tenant_index[:, None] == jnp.arange(tenants, dtype=jnp.int32)[None, :]


def reference(tokens, q_weight, pool_down, pool_up, block_units, adapter_ids, location):
    def one_group(group_index):
        row_block = lax.dynamic_slice_in_dim(tokens, group_index * GROUP, GROUP, 0)
        slot_ids = location[adapter_ids[group_index]]
        down_flat = pool_down[slot_ids].reshape(TEN * R, D)
        up_flat = pool_up[slot_ids].reshape(TEN * R, QOUT)
        base_projection = jnp.dot(row_block, q_weight, preferred_element_type=jnp.float32)
        wide_part = jnp.dot(row_block, down_flat.T, preferred_element_type=jnp.float32).reshape(GROUP, TEN, R)
        tenant_masks = tenant_mask(block_units[group_index], GROUP, TEN)
        low_rank = jnp.sum(jnp.where(tenant_masks[:, :, None], wide_part, jnp.zeros((), jnp.float32)), axis=1)
        low_rank = low_rank.astype(jnp.bfloat16)
        low_wide = jnp.where(tenant_masks[:, :, None], low_rank[:, None, :], jnp.zeros((), jnp.bfloat16))
        adapter_contribution = jnp.dot(low_wide.reshape(GROUP, TEN * R), up_flat, preferred_element_type=jnp.float32)
        return (base_projection + adapter_scale * adapter_contribution).astype(jnp.bfloat16)

    query_output = lax.map(one_group, jnp.arange(GROUPS, dtype=jnp.int32))
    return query_output.reshape(TOKENS, QOUT)
```

```python
import jax
import jax.numpy as jnp
from jax import lax
from jax.sharding import PartitionSpec as P

adapter_scale = 0.5


def tenant_mask(pool_unit_row, group_rows, tenants):
    block_ends = 16 * jnp.cumsum(pool_unit_row)
    positions = jnp.arange(group_rows, dtype=jnp.int32)
    tenant_index = jnp.sum((positions[:, None] >= block_ends[None, :]).astype(jnp.int32), axis=1)
    return tenant_index[:, None] == jnp.arange(tenants, dtype=jnp.int32)[None, :]


def on_device(tokens, q_weight, pool_down, pool_up, block_units, adapter_ids, location):
    my_group = lax.axis_index("dp")
    groups = adapter_ids.shape[0]
    tenants = adapter_ids.shape[1]
    pool_dev = pool_down.shape[0]
    rank_size = pool_down.shape[1]
    local_width = pool_down.shape[2]
    columns = q_weight.shape[1]

    slot_ids = jnp.take(location, adapter_ids, axis=0)
    slot_shard = slot_ids // pool_dev
    slot_row = slot_ids % pool_dev

    from_me = slot_shard == my_group
    send_row = jnp.sum(jnp.where(from_me, slot_row, 0), axis=1)
    both = jnp.concatenate([pool_down, pool_up], axis=1)
    send = jnp.take(both, send_row, axis=0)
    recv = lax.all_to_all(send, "dp", 0, 0, tiled=True)
    my_src = lax.dynamic_index_in_dim(slot_shard, my_group, 0, keepdims=False)
    panels = jnp.take(recv, my_src, axis=0)
    down_flat = panels[:, :rank_size, :].reshape(tenants * rank_size, local_width)
    up_flat = panels[:, rank_size:, :].reshape(tenants * rank_size, columns)

    width_start = lax.axis_index("tensor") * local_width
    row_block = lax.all_gather(tokens, "tensor", axis=0, tiled=True)
    base_projection = jnp.dot(row_block, q_weight, preferred_element_type=jnp.float32)
    local_cols = lax.dynamic_slice_in_dim(row_block, width_start, local_width, 1)
    wide_part = lax.dot_general(
        local_cols, down_flat, (((1,), (1,)), ((), ())), preferred_element_type=jnp.float32
    )
    group_rows = wide_part.shape[0]
    wide_part = wide_part.reshape(group_rows, tenants, rank_size)
    pool_unit_row = lax.dynamic_index_in_dim(block_units, my_group, 0, keepdims=False)
    tenant_masks = tenant_mask(pool_unit_row, group_rows, tenants)
    partial_low = jnp.sum(
        jnp.where(tenant_masks[:, :, None], wide_part, jnp.zeros((), jnp.float32)), axis=1
    )
    low_part = lax.psum_scatter(partial_low, "tensor", scatter_dimension=0, tiled=True)
    low_rank = lax.all_gather(low_part, "tensor", axis=0, tiled=True).astype(jnp.bfloat16)
    low_wide = jnp.where(
        tenant_masks[:, :, None], low_rank[:, None, :], jnp.zeros((), jnp.bfloat16)
    )
    adapter_contribution = jnp.dot(
        low_wide.reshape(group_rows, tenants * rank_size),
        up_flat,
        preferred_element_type=jnp.float32,
    )
    return (base_projection + adapter_scale * adapter_contribution).astype(jnp.bfloat16)


def solution(mesh):
    placed = (
        P(("dp", "tensor"), None),
        P(None, "tensor"),
        P("dp", None, "tensor"),
        P("dp", None, "tensor"),
        P(),
        P(),
        P(),
    )
    return jax.shard_map(
        on_device, mesh=mesh, in_specs=placed, out_specs=P("dp", "tensor"), check_vma=False
    )
```

```python
import jax
import jax.numpy as jnp
from jax import lax
from jax.sharding import PartitionSpec as P

adapter_scale = 0.5


def tenant_mask(pool_unit_row, group_rows, tenants):
    block_ends = 16 * jnp.cumsum(pool_unit_row)
    positions = jnp.arange(group_rows, dtype=jnp.int32)
    tenant_index = jnp.sum((positions[:, None] >= block_ends[None, :]).astype(jnp.int32), axis=1)
    return tenant_index[:, None] == jnp.arange(tenants, dtype=jnp.int32)[None, :]


def tensor_sum(value, members):
    step = 1
    while step < members:
        pairs = [(i, i ^ step) for i in range(members)]
        value = value + lax.ppermute(value, "tensor", pairs)
        step *= 2
    return value


def on_device(tokens, q_weight, pool_down, pool_up, block_units, adapter_ids, location):
    my_group = lax.axis_index("dp")
    groups = adapter_ids.shape[0]
    tenants = adapter_ids.shape[1]
    pool_dev = pool_down.shape[0]
    rank_size = pool_down.shape[1]
    local_width = pool_down.shape[2]
    columns = q_weight.shape[1]

    slot_ids = jnp.take(location, adapter_ids, axis=0)
    slot_shard = slot_ids // pool_dev
    slot_row = slot_ids % pool_dev

    from_me = slot_shard == my_group
    send_row = jnp.sum(jnp.where(from_me, slot_row, 0), axis=1)
    both = jnp.concatenate([pool_down, pool_up], axis=1)
    send = jnp.take(both, send_row, axis=0)
    recv = lax.all_to_all(send, "dp", 0, 0, tiled=True)
    my_src = lax.dynamic_index_in_dim(slot_shard, my_group, 0, keepdims=False)
    panels = jnp.take(recv, my_src, axis=0)
    down_flat = panels[:, :rank_size, :].reshape(tenants * rank_size, local_width)
    up_flat = panels[:, rank_size:, :].reshape(tenants * rank_size, columns)

    width_start = lax.axis_index("tensor") * local_width
    row_block = lax.all_gather(tokens, "tensor", axis=0, tiled=True)
    base_projection = jnp.dot(row_block, q_weight, preferred_element_type=jnp.float32)
    local_cols = lax.dynamic_slice_in_dim(row_block, width_start, local_width, 1)
    wide_part = lax.dot_general(
        local_cols, down_flat, (((1,), (1,)), ((), ())), preferred_element_type=jnp.float32
    )
    group_rows = wide_part.shape[0]
    wide_part = wide_part.reshape(group_rows, tenants, rank_size)
    pool_unit_row = lax.dynamic_index_in_dim(block_units, my_group, 0, keepdims=False)
    tenant_masks = tenant_mask(pool_unit_row, group_rows, tenants)
    partial_low = jnp.sum(
        jnp.where(tenant_masks[:, :, None], wide_part, jnp.zeros((), jnp.float32)), axis=1
    )
    low_rank = tensor_sum(partial_low, lax.axis_size("tensor")).astype(jnp.bfloat16)
    low_wide = jnp.where(
        tenant_masks[:, :, None], low_rank[:, None, :], jnp.zeros((), jnp.bfloat16)
    )
    adapter_contribution = jnp.dot(
        low_wide.reshape(group_rows, tenants * rank_size),
        up_flat,
        preferred_element_type=jnp.float32,
    )
    return (base_projection + adapter_scale * adapter_contribution).astype(jnp.bfloat16)


def solution(mesh):
    placed = (
        P(("dp", "tensor"), None),
        P(None, "tensor"),
        P("dp", None, "tensor"),
        P("dp", None, "tensor"),
        P(),
        P(),
        P(),
    )
    return jax.shard_map(
        on_device, mesh=mesh, in_specs=placed, out_specs=P("dp", "tensor"), check_vma=False
    )
```

```python
import jax
import jax.numpy as jnp
from jax import lax
from jax.sharding import PartitionSpec as P

adapter_scale = 0.5


def tenant_mask(pool_unit_row, group_rows, tenants):
    block_ends = 16 * jnp.cumsum(pool_unit_row)
    positions = jnp.arange(group_rows, dtype=jnp.int32)
    tenant_index = jnp.sum((positions[:, None] >= block_ends[None, :]).astype(jnp.int32), axis=1)
    return tenant_index[:, None] == jnp.arange(tenants, dtype=jnp.int32)[None, :]


def tensor_sum(value, members):
    step = 1
    while step < members:
        pairs = [(i, i ^ step) for i in range(members)]
        value = value + lax.ppermute(value, "tensor", pairs)
        step *= 2
    return value


def on_device(tokens, q_weight, pool_down, pool_up, block_units, adapter_ids, location):
    my_group = lax.axis_index("dp")
    groups = adapter_ids.shape[0]
    tenants = adapter_ids.shape[1]
    pool_dev = pool_down.shape[0]
    rank_size = pool_down.shape[1]
    local_width = pool_down.shape[2]
    columns = q_weight.shape[1]

    slot_ids = jnp.take(location, adapter_ids, axis=0)
    slot_shard = slot_ids // pool_dev
    slot_row = slot_ids % pool_dev

    from_me = slot_shard == my_group
    send_row = jnp.sum(jnp.where(from_me, slot_row, 0), axis=1)
    both = jnp.concatenate([pool_down, pool_up], axis=1)
    send = jnp.take(both, send_row, axis=0)
    recv = lax.all_to_all(send, "dp", 0, 0, tiled=True)
    my_src = lax.dynamic_index_in_dim(slot_shard, my_group, 0, keepdims=False)
    panels = jnp.take(recv, my_src, axis=0)
    down_flat = panels[:, :rank_size, :].reshape(tenants * rank_size, local_width)
    up_flat = panels[:, rank_size:, :].reshape(tenants * rank_size, columns)

    tensor_at = lax.axis_index("tensor")
    members = lax.axis_size("tensor")
    ring = members // 2
    half = tensor_at // ring
    ring_at = tensor_at % ring
    width_start = tensor_at * local_width
    shard_rows = tokens.shape[0]
    group_rows = shard_rows * members
    pool_unit_row = lax.dynamic_index_in_dim(block_units, my_group, 0, keepdims=False)
    block_ends = 16 * jnp.cumsum(pool_unit_row)

    swap = [(i, i ^ ring) for i in range(members)]
    from_right = [(i, (i // ring) * ring + (i % ring - 1) % ring) for i in range(members)]
    from_left = [(i, (i // ring) * ring + (i % ring + 1) % ring) for i in range(members)]

    def ring_pieces(own):
        pieces = [own] + [None] * (ring - 1)
        right, left = own, own
        for step in range(1, ring // 2):
            right = lax.ppermute(right, "tensor", from_right)
            left = lax.ppermute(left, "tensor", from_left)
            pieces[step], pieces[ring - step] = right, left
        cut = shard_rows // 2
        far_right = lax.ppermute(right[:cut], "tensor", from_right)
        far_left = lax.ppermute(left[cut:], "tensor", from_left)
        pieces[ring // 2] = jnp.concatenate([far_right, far_left], axis=0)
        return pieces

    partner = lax.ppermute(tokens, "tensor", swap)
    own_pieces = ring_pieces(tokens)
    partner_pieces = ring_pieces(partner)

    tenant_ids = jnp.arange(tenants, dtype=jnp.int32)

    def piece_work(piece, piece_half, step):
        first_row = (piece_half * ring + (ring_at + step) % ring) * shard_rows
        positions = first_row + jnp.arange(shard_rows, dtype=jnp.int32)
        tenant_index = jnp.sum((positions[:, None] >= block_ends[None, :]).astype(jnp.int32), axis=1)
        masks = tenant_index[:, None] == tenant_ids[None, :]
        base = jnp.dot(piece, q_weight, preferred_element_type=jnp.float32)
        cols = lax.dynamic_slice_in_dim(piece, width_start, local_width, 1)
        wide = lax.dot_general(
            cols, down_flat, (((1,), (1,)), ((), ())), preferred_element_type=jnp.float32
        ).reshape(shard_rows, tenants, rank_size)
        low = jnp.sum(jnp.where(masks[:, :, None], wide, jnp.zeros((), jnp.float32)), axis=1)
        return base, low

    own_work = [piece_work(p, half, k) for k, p in enumerate(own_pieces)]
    partner_work = [piece_work(p, 1 - half, k) for k, p in enumerate(partner_pieces)]

    def to_group_order(own_list, partner_list):
        def roll(stacked):
            doubled = jnp.concatenate([stacked, stacked], axis=0)
            return lax.dynamic_slice_in_dim(doubled, (ring - ring_at) % ring, ring, 0)
        own_abs = roll(jnp.stack(own_list))
        partner_abs = roll(jnp.stack(partner_list))
        ordered = jnp.where(
            half == 0, jnp.stack([own_abs, partner_abs]), jnp.stack([partner_abs, own_abs])
        )
        return ordered.reshape((group_rows,) + own_list[0].shape[1:])

    base_projection = to_group_order([w[0] for w in own_work], [w[0] for w in partner_work])
    partial_low = to_group_order([w[1] for w in own_work], [w[1] for w in partner_work])
    positions = jnp.arange(group_rows, dtype=jnp.int32)
    tenant_index = jnp.sum((positions[:, None] >= block_ends[None, :]).astype(jnp.int32), axis=1)
    tenant_masks = tenant_index[:, None] == tenant_ids[None, :]
    low_rank = tensor_sum(partial_low, members).astype(jnp.bfloat16)
    low_wide = jnp.where(
        tenant_masks[:, :, None], low_rank[:, None, :], jnp.zeros((), jnp.bfloat16)
    )
    adapter_contribution = jnp.dot(
        low_wide.reshape(group_rows, tenants * rank_size),
        up_flat,
        preferred_element_type=jnp.float32,
    )
    return (base_projection + adapter_scale * adapter_contribution).astype(jnp.bfloat16)


def solution(mesh):
    placed = (
        P(("dp", "tensor"), None),
        P(None, "tensor"),
        P("dp", None, "tensor"),
        P("dp", None, "tensor"),
        P(),
        P(),
        P(),
    )
    return jax.shard_map(
        on_device, mesh=mesh, in_specs=placed, out_specs=P("dp", "tensor"), check_vma=False
    )
```

```python
import jax
import jax.numpy as jnp
from jax import lax
from jax.sharding import PartitionSpec as P

adapter_scale = 0.5


def tenant_mask(pool_unit_row, group_rows, tenants):
    block_ends = 16 * jnp.cumsum(pool_unit_row)
    positions = jnp.arange(group_rows, dtype=jnp.int32)
    tenant_index = jnp.sum((positions[:, None] >= block_ends[None, :]).astype(jnp.int32), axis=1)
    return tenant_index[:, None] == jnp.arange(tenants, dtype=jnp.int32)[None, :]


def tensor_sum(value, members):
    step = 1
    while step < members:
        pairs = [(i, i ^ step) for i in range(members)]
        value = value + lax.ppermute(value, "tensor", pairs)
        step *= 2
    return value


def on_device(tokens, q_weight, pool_down, pool_up, block_units, adapter_ids, location):
    my_group = lax.axis_index("dp")
    groups = adapter_ids.shape[0]
    tenants = adapter_ids.shape[1]
    pool_dev = pool_down.shape[0]
    rank_size = pool_down.shape[1]
    local_width = pool_down.shape[2]
    columns = q_weight.shape[1]

    slot_ids = jnp.take(location, adapter_ids, axis=0)
    slot_shard = slot_ids // pool_dev
    slot_row = slot_ids % pool_dev

    from_me = slot_shard == my_group
    send_row = jnp.sum(jnp.where(from_me, slot_row, 0), axis=1)
    both = jnp.concatenate([pool_down, pool_up], axis=1)
    send = jnp.take(both, send_row, axis=0)
    recv = lax.all_to_all(send, "dp", 0, 0, tiled=True)
    my_src = lax.dynamic_index_in_dim(slot_shard, my_group, 0, keepdims=False)
    panels = jnp.take(recv, my_src, axis=0)
    down_flat = panels[:, :rank_size, :].reshape(tenants * rank_size, local_width)
    up_flat = panels[:, rank_size:, :].reshape(tenants * rank_size, columns)

    tensor_at = lax.axis_index("tensor")
    members = lax.axis_size("tensor")
    ring = members // 2
    half = tensor_at // ring
    ring_at = tensor_at % ring
    width_start = tensor_at * local_width
    shard_rows = tokens.shape[0]
    group_rows = shard_rows * members
    pool_unit_row = lax.dynamic_index_in_dim(block_units, my_group, 0, keepdims=False)
    block_ends = 16 * jnp.cumsum(pool_unit_row)

    swap = [(i, i ^ ring) for i in range(members)]
    from_right = [(i, (i // ring) * ring + (i % ring - 1) % ring) for i in range(members)]
    from_left = [(i, (i // ring) * ring + (i % ring + 1) % ring) for i in range(members)]

    def ring_pieces(own):
        pieces = [own] + [None] * (ring - 1)
        right, left = own, own
        for step in range(1, ring // 2):
            right = lax.ppermute(right, "tensor", from_right)
            left = lax.ppermute(left, "tensor", from_left)
            pieces[step], pieces[ring - step] = right, left
        cut = shard_rows // 2
        far_right = lax.ppermute(right[:cut], "tensor", from_right)
        far_left = lax.ppermute(left[cut:], "tensor", from_left)
        pieces[ring // 2] = jnp.concatenate([far_right, far_left], axis=0)
        return pieces

    partner = lax.ppermute(tokens, "tensor", swap)
    own_pieces = ring_pieces(tokens)
    partner_pieces = ring_pieces(partner)

    tenant_ids = jnp.arange(tenants, dtype=jnp.int32)

    arrivals = [
        [("own", 0)],
        [("own", 1), ("own", ring - 1), ("partner", 0)],
    ]
    for step in range(2, ring // 2):
        arrivals.append([("own", step), ("own", ring - step), ("partner", step - 1), ("partner", ring - step + 1)])
    arrivals.append([("own", ring // 2), ("partner", ring // 2 - 1), ("partner", ring // 2 + 1)])
    arrivals.append([("partner", ring // 2)])
    pieces = {"own": own_pieces, "partner": partner_pieces}
    base_of = {"own": [None] * ring, "partner": [None] * ring}
    for batch in arrivals:
        stacked = jnp.concatenate([pieces[side][k] for side, k in batch], axis=0)
        product = jnp.dot(stacked, q_weight, preferred_element_type=jnp.float32)
        for i, (side, k) in enumerate(batch):
            base_of[side][k] = product[i * shard_rows:(i + 1) * shard_rows]

    def to_group_order(own_list, partner_list):
        def roll(stacked):
            doubled = jnp.concatenate([stacked, stacked], axis=0)
            return lax.dynamic_slice_in_dim(doubled, (ring - ring_at) % ring, ring, 0)
        own_abs = roll(jnp.stack(own_list))
        partner_abs = roll(jnp.stack(partner_list))
        ordered = jnp.where(
            half == 0, jnp.stack([own_abs, partner_abs]), jnp.stack([partner_abs, own_abs])
        )
        return ordered.reshape((group_rows,) + own_list[0].shape[1:])

    base_projection = to_group_order(base_of["own"], base_of["partner"])

    local_cols = lax.all_to_all(tokens, "tensor", 1, 0, tiled=True)
    wide_part = lax.dot_general(
        local_cols, down_flat, (((1,), (1,)), ((), ())), preferred_element_type=jnp.float32
    ).reshape(group_rows, tenants, rank_size)
    positions = jnp.arange(group_rows, dtype=jnp.int32)
    tenant_index = jnp.sum((positions[:, None] >= block_ends[None, :]).astype(jnp.int32), axis=1)
    tenant_masks = tenant_index[:, None] == tenant_ids[None, :]
    partial_low = jnp.sum(
        jnp.where(tenant_masks[:, :, None], wide_part, jnp.zeros((), jnp.float32)), axis=1
    )
    low_rank = tensor_sum(partial_low, members).astype(jnp.bfloat16)
    low_wide = jnp.where(
        tenant_masks[:, :, None], low_rank[:, None, :], jnp.zeros((), jnp.bfloat16)
    )
    adapter_contribution = jnp.dot(
        low_wide.reshape(group_rows, tenants * rank_size),
        up_flat,
        preferred_element_type=jnp.float32,
    )
    return (base_projection + adapter_scale * adapter_contribution).astype(jnp.bfloat16)


def solution(mesh):
    placed = (
        P(("dp", "tensor"), None),
        P(None, "tensor"),
        P("dp", None, "tensor"),
        P("dp", None, "tensor"),
        P(),
        P(),
        P(),
    )
    return jax.shard_map(
        on_device, mesh=mesh, in_specs=placed, out_specs=P("dp", "tensor"), check_vma=False
    )
```

```python
import jax
import jax.numpy as jnp
from jax import lax
from jax.sharding import PartitionSpec as P

adapter_scale = 0.5


def tenant_mask(pool_unit_row, group_rows, tenants):
    block_ends = 16 * jnp.cumsum(pool_unit_row)
    positions = jnp.arange(group_rows, dtype=jnp.int32)
    tenant_index = jnp.sum((positions[:, None] >= block_ends[None, :]).astype(jnp.int32), axis=1)
    return tenant_index[:, None] == jnp.arange(tenants, dtype=jnp.int32)[None, :]


def tensor_sum(value, members):
    step = 1
    while step < members:
        pairs = [(i, i ^ step) for i in range(members)]
        value = value + lax.ppermute(value, "tensor", pairs)
        step *= 2
    return value


def on_device(tokens, q_weight, pool_down, pool_up, block_units, adapter_ids, location):
    my_group = lax.axis_index("dp")
    groups = adapter_ids.shape[0]
    tenants = adapter_ids.shape[1]
    pool_dev = pool_down.shape[0]
    rank_size = pool_down.shape[1]
    local_width = pool_down.shape[2]
    columns = q_weight.shape[1]

    slot_ids = jnp.take(location, adapter_ids, axis=0)
    slot_shard = slot_ids // pool_dev
    slot_row = slot_ids % pool_dev

    from_me = slot_shard == my_group
    send_row = jnp.sum(jnp.where(from_me, slot_row, 0), axis=1)
    both = jnp.concatenate([pool_down, pool_up], axis=1)
    send = jnp.take(both, send_row, axis=0)
    recv = lax.all_to_all(send, "dp", 0, 0, tiled=True)
    my_src = lax.dynamic_index_in_dim(slot_shard, my_group, 0, keepdims=False)
    panels = jnp.take(recv, my_src, axis=0)

    tensor_at = lax.axis_index("tensor")
    members = lax.axis_size("tensor")
    ring = members // 2
    half = tensor_at // ring
    ring_at = tensor_at % ring
    width_start = tensor_at * local_width
    shard_rows = tokens.shape[0]
    group_rows = shard_rows * members
    pool_unit_row = lax.dynamic_index_in_dim(block_units, my_group, 0, keepdims=False)
    block_ends = 16 * jnp.cumsum(pool_unit_row)

    swap = [(i, i ^ ring) for i in range(members)]
    from_right = [(i, (i // ring) * ring + (i % ring - 1) % ring) for i in range(members)]
    from_left = [(i, (i // ring) * ring + (i % ring + 1) % ring) for i in range(members)]

    def hop(value, pairs):
        return lax.ppermute(value, "tensor", pairs)

    tenant_ids = jnp.arange(tenants, dtype=jnp.int32)
    positions = jnp.arange(group_rows, dtype=jnp.int32)
    tenant_index = jnp.sum((positions[:, None] >= block_ends[None, :]).astype(jnp.int32), axis=1)
    tenant_masks = tenant_index[:, None] == tenant_ids[None, :]

    local_cols = lax.all_to_all(tokens, "tensor", 1, 0, tiled=True)

    def partial_of(cols):
        wide = lax.dot_general(
            cols, down_flat, (((1,), (1,)), ((), ())), preferred_element_type=jnp.float32
        ).reshape(group_rows, tenants, rank_size)
        return jnp.sum(jnp.where(tenant_masks[:, :, None], wide, jnp.zeros((), jnp.float32)), axis=1)

    sum_steps = [ring]
    step = ring // 2
    while step >= 1:
        sum_steps.append(step)
        step //= 2

    def sum_step(value, mask):
        return value + hop(value, [(i, i ^ mask) for i in range(members)])

    own_pieces = [tokens] + [None] * (ring - 1)
    partner_pieces = [None] * ring
    cut = shard_rows // 2
    partner = hop(tokens, swap)
    own_right = hop(tokens, from_right)
    own_left = hop(tokens, from_left)
    partner, own_right, own_left = lax.optimization_barrier((partner, own_right, own_left))
    own_pieces[1], own_pieces[ring - 1] = own_right, own_left
    partner_pieces[0] = partner
    partner_right, partner_left = partner, partner
    low_sum = None
    for step in range(2, ring // 2 + 2):
        moved = []
        if step < ring // 2:
            moved += [hop(own_right, from_right), hop(own_left, from_left)]
        elif step == ring // 2:
            moved += [hop(own_right[:cut], from_right), hop(own_left[cut:], from_left)]
        if step - 1 < ring // 2:
            moved += [hop(partner_right, from_right), hop(partner_left, from_left)]
        else:
            moved += [hop(partner_right[:cut], from_right), hop(partner_left[cut:], from_left)]
        if low_sum is None:
            extra = (local_cols, panels)
        else:
            extra = (sum_step(low_sum, sum_steps.pop(0)),)
        moved, extra = lax.optimization_barrier((moved, extra))
        if low_sum is None:
            local_cols, panels = extra
            down_flat = panels[:, :rank_size, :].reshape(tenants * rank_size, local_width)
            up_flat = panels[:, rank_size:, :].reshape(tenants * rank_size, columns)
            low_sum = partial_of(local_cols)
        else:
            low_sum = extra[0]
        if step < ring // 2:
            own_right, own_left = moved[0], moved[1]
            own_pieces[step], own_pieces[ring - step] = own_right, own_left
            moved = moved[2:]
        elif step == ring // 2:
            own_pieces[step] = jnp.concatenate(moved[:2], axis=0)
            moved = moved[2:]
        if step - 1 < ring // 2:
            partner_right, partner_left = moved
            partner_pieces[step - 1], partner_pieces[ring - step + 1] = partner_right, partner_left
        else:
            partner_pieces[ring // 2] = jnp.concatenate(moved, axis=0)
    for mask in sum_steps:
        low_sum = sum_step(low_sum, mask)

    arrivals = [
        [("own", 0)],
        [("own", 1), ("own", ring - 1), ("partner", 0)],
    ]
    for step in range(2, ring // 2):
        arrivals.append([("own", step), ("own", ring - step), ("partner", step - 1), ("partner", ring - step + 1)])
    arrivals.append([("own", ring // 2), ("partner", ring // 2 - 1), ("partner", ring // 2 + 1)])
    arrivals.append([("partner", ring // 2)])
    pieces = {"own": own_pieces, "partner": partner_pieces}
    base_of = {"own": [None] * ring, "partner": [None] * ring}
    for batch in arrivals:
        stacked = jnp.concatenate([pieces[side][k] for side, k in batch], axis=0)
        product = jnp.dot(stacked, q_weight, preferred_element_type=jnp.float32)
        for i, (side, k) in enumerate(batch):
            base_of[side][k] = product[i * shard_rows:(i + 1) * shard_rows]

    def to_group_order(own_list, partner_list):
        def roll(stacked):
            doubled = jnp.concatenate([stacked, stacked], axis=0)
            return lax.dynamic_slice_in_dim(doubled, (ring - ring_at) % ring, ring, 0)
        own_abs = roll(jnp.stack(own_list))
        partner_abs = roll(jnp.stack(partner_list))
        ordered = jnp.where(
            half == 0, jnp.stack([own_abs, partner_abs]), jnp.stack([partner_abs, own_abs])
        )
        return ordered.reshape((group_rows,) + own_list[0].shape[1:])

    base_projection = to_group_order(base_of["own"], base_of["partner"])
    low_rank = low_sum.astype(jnp.bfloat16)
    low_wide = jnp.where(
        tenant_masks[:, :, None], low_rank[:, None, :], jnp.zeros((), jnp.bfloat16)
    )
    adapter_contribution = jnp.dot(
        low_wide.reshape(group_rows, tenants * rank_size),
        up_flat,
        preferred_element_type=jnp.float32,
    )
    return (base_projection + adapter_scale * adapter_contribution).astype(jnp.bfloat16)


def solution(mesh):
    placed = (
        P(("dp", "tensor"), None),
        P(None, "tensor"),
        P("dp", None, "tensor"),
        P("dp", None, "tensor"),
        P(),
        P(),
        P(),
    )
    return jax.shard_map(
        on_device, mesh=mesh, in_specs=placed, out_specs=P("dp", "tensor"), check_vma=False
    )
```

```python
import jax
import jax.numpy as jnp
from jax import lax
from jax.sharding import PartitionSpec as P

adapter_scale = 0.5


def tenant_mask(pool_unit_row, group_rows, tenants):
    block_ends = 16 * jnp.cumsum(pool_unit_row)
    positions = jnp.arange(group_rows, dtype=jnp.int32)
    tenant_index = jnp.sum((positions[:, None] >= block_ends[None, :]).astype(jnp.int32), axis=1)
    return tenant_index[:, None] == jnp.arange(tenants, dtype=jnp.int32)[None, :]


def tensor_sum(value, members):
    step = 1
    while step < members:
        pairs = [(i, i ^ step) for i in range(members)]
        value = value + lax.ppermute(value, "tensor", pairs)
        step *= 2
    return value


def on_device(tokens, q_weight, pool_down, pool_up, block_units, adapter_ids, location):
    my_group = lax.axis_index("dp")
    groups = adapter_ids.shape[0]
    tenants = adapter_ids.shape[1]
    pool_dev = pool_down.shape[0]
    rank_size = pool_down.shape[1]
    local_width = pool_down.shape[2]
    columns = q_weight.shape[1]

    slot_ids = jnp.take(location, adapter_ids, axis=0)
    slot_shard = slot_ids // pool_dev
    slot_row = slot_ids % pool_dev

    from_me = slot_shard == my_group
    send_row = jnp.sum(jnp.where(from_me, slot_row, 0), axis=1)
    both = jnp.concatenate([pool_down, pool_up], axis=1)
    send = jnp.take(both, send_row, axis=0)
    recv = lax.all_to_all(send, "dp", 0, 0, tiled=True)
    my_src = lax.dynamic_index_in_dim(slot_shard, my_group, 0, keepdims=False)
    panels = jnp.take(recv, my_src, axis=0)

    tensor_at = lax.axis_index("tensor")
    members = lax.axis_size("tensor")
    ring = members // 2
    half = tensor_at // ring
    ring_at = tensor_at % ring
    width_start = tensor_at * local_width
    shard_rows = tokens.shape[0]
    group_rows = shard_rows * members
    pool_unit_row = lax.dynamic_index_in_dim(block_units, my_group, 0, keepdims=False)
    block_ends = 16 * jnp.cumsum(pool_unit_row)

    swap = [(i, i ^ ring) for i in range(members)]
    from_right = [(i, (i // ring) * ring + (i % ring - 1) % ring) for i in range(members)]
    from_left = [(i, (i // ring) * ring + (i % ring + 1) % ring) for i in range(members)]

    def hop(value, pairs):
        return lax.ppermute(value, "tensor", pairs)

    tenant_ids = jnp.arange(tenants, dtype=jnp.int32)
    positions = jnp.arange(group_rows, dtype=jnp.int32)
    tenant_index = jnp.sum((positions[:, None] >= block_ends[None, :]).astype(jnp.int32), axis=1)
    tenant_masks = tenant_index[:, None] == tenant_ids[None, :]

    def sum_step(value, mask):
        return value + hop(value, [(i, i ^ mask) for i in range(members)])

    own_pieces = [tokens] + [None] * (ring - 1)
    partner_pieces = [None] * ring
    cut = shard_rows // 2
    partner = hop(tokens, swap)
    own_right = hop(tokens, from_right)
    own_left = hop(tokens, from_left)
    partner, own_right, own_left = lax.optimization_barrier((partner, own_right, own_left))
    own_pieces[1], own_pieces[ring - 1] = own_right, own_left
    partner_pieces[0] = partner
    partner_right, partner_left = partner, partner
    for step in range(2, ring // 2 + 2):
        moved = []
        if step < ring // 2:
            moved += [hop(own_right, from_right), hop(own_left, from_left)]
        elif step == ring // 2:
            moved += [hop(own_right[:cut], from_right), hop(own_left[cut:], from_left)]
        if step - 1 < ring // 2:
            moved += [hop(partner_right, from_right), hop(partner_left, from_left)]
        else:
            moved += [hop(partner_right[:cut], from_right), hop(partner_left[cut:], from_left)]
        moved = lax.optimization_barrier(moved)
        if step < ring // 2:
            own_right, own_left = moved[0], moved[1]
            own_pieces[step], own_pieces[ring - step] = own_right, own_left
            moved = moved[2:]
        elif step == ring // 2:
            own_pieces[step] = jnp.concatenate(moved[:2], axis=0)
            moved = moved[2:]
        if step - 1 < ring // 2:
            partner_right, partner_left = moved
            partner_pieces[step - 1], partner_pieces[ring - step + 1] = partner_right, partner_left
        else:
            partner_pieces[ring // 2] = jnp.concatenate(moved, axis=0)
    arrivals = [
        [("own", 0)],
        [("own", 1), ("own", ring - 1), ("partner", 0)],
    ]
    for step in range(2, ring // 2):
        arrivals.append([("own", step), ("own", ring - step), ("partner", step - 1), ("partner", ring - step + 1)])
    arrivals.append([("own", ring // 2), ("partner", ring // 2 - 1), ("partner", ring // 2 + 1)])
    arrivals.append([("partner", ring // 2)])
    pieces = {"own": own_pieces, "partner": partner_pieces}
    down_flat = panels[:, :rank_size, :].reshape(tenants * rank_size, local_width)
    up_flat = panels[:, rank_size:, :].reshape(tenants * rank_size, columns)
    base_of = {"own": [None] * ring, "partner": [None] * ring}
    wide_of = {"own": [None] * ring, "partner": [None] * ring}
    for batch in arrivals:
        stacked = jnp.concatenate([pieces[side][k] for side, k in batch], axis=0)
        product = jnp.dot(stacked, q_weight, preferred_element_type=jnp.float32)
        cols = lax.dynamic_slice_in_dim(stacked, width_start, local_width, 1)
        wide = lax.dot_general(
            cols, down_flat, (((1,), (1,)), ((), ())), preferred_element_type=jnp.float32
        )
        for i, (side, k) in enumerate(batch):
            base_of[side][k] = product[i * shard_rows:(i + 1) * shard_rows]
            wide_of[side][k] = wide[i * shard_rows:(i + 1) * shard_rows]

    def to_group_order(own_list, partner_list):
        def roll(stacked):
            doubled = jnp.concatenate([stacked, stacked], axis=0)
            return lax.dynamic_slice_in_dim(doubled, (ring - ring_at) % ring, ring, 0)
        own_abs = roll(jnp.stack(own_list))
        partner_abs = roll(jnp.stack(partner_list))
        ordered = jnp.where(
            half == 0, jnp.stack([own_abs, partner_abs]), jnp.stack([partner_abs, own_abs])
        )
        return ordered.reshape((group_rows,) + own_list[0].shape[1:])

    base_projection = to_group_order(base_of["own"], base_of["partner"])
    wide_part = to_group_order(wide_of["own"], wide_of["partner"]).reshape(group_rows, tenants, rank_size)
    partial_low = jnp.sum(
        jnp.where(tenant_masks[:, :, None], wide_part, jnp.zeros((), jnp.float32)), axis=1
    )
    low_sum = partial_low
    step = 1
    while step < members:
        low_sum = sum_step(low_sum, step)
        step *= 2
    low_rank = low_sum.astype(jnp.bfloat16)
    low_wide = jnp.where(
        tenant_masks[:, :, None], low_rank[:, None, :], jnp.zeros((), jnp.bfloat16)
    )
    adapter_contribution = jnp.dot(
        low_wide.reshape(group_rows, tenants * rank_size),
        up_flat,
        preferred_element_type=jnp.float32,
    )
    return (base_projection + adapter_scale * adapter_contribution).astype(jnp.bfloat16)


def solution(mesh):
    placed = (
        P(("dp", "tensor"), None),
        P(None, "tensor"),
        P("dp", None, "tensor"),
        P("dp", None, "tensor"),
        P(),
        P(),
        P(),
    )
    return jax.shard_map(
        on_device, mesh=mesh, in_specs=placed, out_specs=P("dp", "tensor"), check_vma=False
    )
```

```python
import jax
import jax.numpy as jnp
from jax import lax
from jax.sharding import PartitionSpec as P

adapter_scale = 0.5


def tenant_mask(pool_unit_row, group_rows, tenants):
    block_ends = 16 * jnp.cumsum(pool_unit_row)
    positions = jnp.arange(group_rows, dtype=jnp.int32)
    tenant_index = jnp.sum((positions[:, None] >= block_ends[None, :]).astype(jnp.int32), axis=1)
    return tenant_index[:, None] == jnp.arange(tenants, dtype=jnp.int32)[None, :]


def tensor_sum(value, members):
    step = 1
    while step < members:
        pairs = [(i, i ^ step) for i in range(members)]
        value = value + lax.ppermute(value, "tensor", pairs)
        step *= 2
    return value


def on_device(tokens, q_weight, pool_down, pool_up, block_units, adapter_ids, location):
    my_group = lax.axis_index("dp")
    groups = adapter_ids.shape[0]
    tenants = adapter_ids.shape[1]
    pool_dev = pool_down.shape[0]
    rank_size = pool_down.shape[1]
    local_width = pool_down.shape[2]
    columns = q_weight.shape[1]

    slot_ids = jnp.take(location, adapter_ids, axis=0)
    slot_shard = slot_ids // pool_dev
    slot_row = slot_ids % pool_dev

    from_me = slot_shard == my_group
    send_row = jnp.sum(jnp.where(from_me, slot_row, 0), axis=1)
    both = jnp.concatenate([pool_down, pool_up], axis=1)
    send = jnp.take(both, send_row, axis=0)
    recv = lax.all_to_all(send, "dp", 0, 0, tiled=True)
    my_src = lax.dynamic_index_in_dim(slot_shard, my_group, 0, keepdims=False)
    panels = jnp.take(recv, my_src, axis=0)

    tensor_at = lax.axis_index("tensor")
    members = lax.axis_size("tensor")
    ring = members // 2
    half = tensor_at // ring
    ring_at = tensor_at % ring
    width_start = tensor_at * local_width
    shard_rows = tokens.shape[0]
    group_rows = shard_rows * members
    pool_unit_row = lax.dynamic_index_in_dim(block_units, my_group, 0, keepdims=False)
    block_ends = 16 * jnp.cumsum(pool_unit_row)

    swap = [(i, i ^ ring) for i in range(members)]
    from_right = [(i, (i // ring) * ring + (i % ring - 1) % ring) for i in range(members)]
    from_left = [(i, (i // ring) * ring + (i % ring + 1) % ring) for i in range(members)]

    def hop(value, pairs):
        return lax.ppermute(value, "tensor", pairs)

    tenant_ids = jnp.arange(tenants, dtype=jnp.int32)
    positions = jnp.arange(group_rows, dtype=jnp.int32)
    tenant_index = jnp.sum((positions[:, None] >= block_ends[None, :]).astype(jnp.int32), axis=1)
    tenant_masks = tenant_index[:, None] == tenant_ids[None, :]

    local_cols = lax.all_to_all(tokens, "tensor", 1, 0, tiled=True)

    def partial_of(cols):
        wide = lax.dot_general(
            cols, down_flat, (((1,), (1,)), ((), ())), preferred_element_type=jnp.float32
        ).reshape(group_rows, tenants, rank_size)
        return jnp.sum(jnp.where(tenant_masks[:, :, None], wide, jnp.zeros((), jnp.float32)), axis=1)

    sum_steps = [ring]
    step = ring // 2
    while step >= 1:
        sum_steps.append(step)
        step //= 2

    def sum_step(value, mask):
        return value + hop(value, [(i, i ^ mask) for i in range(members)])

    own_pieces = [tokens] + [None] * (ring - 1)
    partner_pieces = [None] * ring
    cut = shard_rows // 2
    partner = hop(tokens, swap)
    own_right = hop(tokens, from_right)
    own_left = hop(tokens, from_left)
    partner, own_right, own_left = lax.optimization_barrier((partner, own_right, own_left))
    own_pieces[1], own_pieces[ring - 1] = own_right, own_left
    partner_pieces[0] = partner
    partner_right, partner_left = partner, partner
    low_sum = None
    for step in range(2, ring // 2 + 2):
        moved = []
        if step < ring // 2:
            moved += [hop(own_right, from_right), hop(own_left, from_left)]
        elif step == ring // 2:
            moved += [hop(own_right[:cut], from_right), hop(own_left[cut:], from_left)]
        if step - 1 < ring // 2:
            moved += [hop(partner_right, from_right), hop(partner_left, from_left)]
        else:
            moved += [hop(partner_right[:cut], from_right), hop(partner_left[cut:], from_left)]
        if low_sum is None:
            extra = (local_cols, panels)
        else:
            low_next = sum_step(low_sum, sum_steps.pop(0))
            if step == ring // 2 + 1:
                while sum_steps:
                    low_next = sum_step(low_next, sum_steps.pop(0))
            extra = (low_next,)
        moved, extra = lax.optimization_barrier((moved, extra))
        if low_sum is None:
            local_cols, panels = extra
            down_flat = panels[:, :rank_size, :].reshape(tenants * rank_size, local_width)
            up_flat = panels[:, rank_size:, :].reshape(tenants * rank_size, columns)
            low_sum = partial_of(local_cols)
        else:
            low_sum = extra[0]
        if step < ring // 2:
            own_right, own_left = moved[0], moved[1]
            own_pieces[step], own_pieces[ring - step] = own_right, own_left
            moved = moved[2:]
        elif step == ring // 2:
            own_pieces[step] = jnp.concatenate(moved[:2], axis=0)
            moved = moved[2:]
        if step - 1 < ring // 2:
            partner_right, partner_left = moved
            partner_pieces[step - 1], partner_pieces[ring - step + 1] = partner_right, partner_left
        else:
            partner_pieces[ring // 2] = jnp.concatenate(moved, axis=0)
    for mask in sum_steps:
        low_sum = sum_step(low_sum, mask)

    arrivals = [
        [("own", 0)],
        [("own", 1), ("own", ring - 1), ("partner", 0)],
    ]
    for step in range(2, ring // 2):
        arrivals.append([("own", step), ("own", ring - step), ("partner", step - 1), ("partner", ring - step + 1)])
    arrivals.append([("own", ring // 2), ("partner", ring // 2 - 1), ("partner", ring // 2 + 1)])
    arrivals.append([("partner", ring // 2)])
    pieces = {"own": own_pieces, "partner": partner_pieces}
    base_of = {"own": [None] * ring, "partner": [None] * ring}
    for batch in arrivals:
        stacked = jnp.concatenate([pieces[side][k] for side, k in batch], axis=0)
        product = jnp.dot(stacked, q_weight, preferred_element_type=jnp.float32)
        for i, (side, k) in enumerate(batch):
            base_of[side][k] = product[i * shard_rows:(i + 1) * shard_rows]

    def to_group_order(own_list, partner_list):
        def roll(stacked):
            doubled = jnp.concatenate([stacked, stacked], axis=0)
            return lax.dynamic_slice_in_dim(doubled, (ring - ring_at) % ring, ring, 0)
        own_abs = roll(jnp.stack(own_list))
        partner_abs = roll(jnp.stack(partner_list))
        ordered = jnp.where(
            half == 0, jnp.stack([own_abs, partner_abs]), jnp.stack([partner_abs, own_abs])
        )
        return ordered.reshape((group_rows,) + own_list[0].shape[1:])

    base_projection = to_group_order(base_of["own"], base_of["partner"])
    low_rank = low_sum.astype(jnp.bfloat16)
    low_wide = jnp.where(
        tenant_masks[:, :, None], low_rank[:, None, :], jnp.zeros((), jnp.bfloat16)
    )
    adapter_contribution = jnp.dot(
        low_wide.reshape(group_rows, tenants * rank_size),
        up_flat,
        preferred_element_type=jnp.float32,
    )
    return (base_projection + adapter_scale * adapter_contribution).astype(jnp.bfloat16)


def solution(mesh):
    placed = (
        P(("dp", "tensor"), None),
        P(None, "tensor"),
        P("dp", None, "tensor"),
        P("dp", None, "tensor"),
        P(),
        P(),
        P(),
    )
    return jax.shard_map(
        on_device, mesh=mesh, in_specs=placed, out_specs=P("dp", "tensor"), check_vma=False
    )
```

```python
import jax
import jax.numpy as jnp
from jax import lax
from jax.sharding import PartitionSpec as P

adapter_scale = 0.5


def tenant_mask(pool_unit_row, group_rows, tenants):
    block_ends = 16 * jnp.cumsum(pool_unit_row)
    positions = jnp.arange(group_rows, dtype=jnp.int32)
    tenant_index = jnp.sum((positions[:, None] >= block_ends[None, :]).astype(jnp.int32), axis=1)
    return tenant_index[:, None] == jnp.arange(tenants, dtype=jnp.int32)[None, :]


def tensor_sum(value, members):
    step = 1
    while step < members:
        pairs = [(i, i ^ step) for i in range(members)]
        value = value + lax.ppermute(value, "tensor", pairs)
        step *= 2
    return value


def on_device(tokens, q_weight, pool_down, pool_up, block_units, adapter_ids, location):
    my_group = lax.axis_index("dp")
    groups = adapter_ids.shape[0]
    tenants = adapter_ids.shape[1]
    pool_dev = pool_down.shape[0]
    rank_size = pool_down.shape[1]
    local_width = pool_down.shape[2]
    columns = q_weight.shape[1]

    slot_ids = jnp.take(location, adapter_ids, axis=0)
    slot_shard = slot_ids // pool_dev
    slot_row = slot_ids % pool_dev

    from_me = slot_shard == my_group
    send_row = jnp.sum(jnp.where(from_me, slot_row, 0), axis=1)
    both = jnp.concatenate([pool_down, pool_up], axis=1)
    send = jnp.take(both, send_row, axis=0)
    recv = lax.all_to_all(send, "dp", 0, 0, tiled=True)
    my_src = lax.dynamic_index_in_dim(slot_shard, my_group, 0, keepdims=False)
    panels = jnp.take(recv, my_src, axis=0)

    tensor_at = lax.axis_index("tensor")
    members = lax.axis_size("tensor")
    ring = members // 2
    half = tensor_at // ring
    ring_at = tensor_at % ring
    width_start = tensor_at * local_width
    shard_rows = tokens.shape[0]
    group_rows = shard_rows * members
    pool_unit_row = lax.dynamic_index_in_dim(block_units, my_group, 0, keepdims=False)
    block_ends = 16 * jnp.cumsum(pool_unit_row)

    swap = [(i, i ^ ring) for i in range(members)]
    from_right = [(i, (i // ring) * ring + (i % ring - 1) % ring) for i in range(members)]
    from_left = [(i, (i // ring) * ring + (i % ring + 1) % ring) for i in range(members)]

    def hop(value, pairs):
        return lax.ppermute(value, "tensor", pairs)

    tenant_ids = jnp.arange(tenants, dtype=jnp.int32)
    positions = jnp.arange(group_rows, dtype=jnp.int32)
    tenant_index = jnp.sum((positions[:, None] >= block_ends[None, :]).astype(jnp.int32), axis=1)
    tenant_masks = tenant_index[:, None] == tenant_ids[None, :]

    local_cols = lax.all_to_all(tokens, "tensor", 1, 0, tiled=True)

    def partial_of(cols):
        wide = lax.dot_general(
            cols, down_flat, (((1,), (1,)), ((), ())), preferred_element_type=jnp.float32
        ).reshape(group_rows, tenants, rank_size)
        return jnp.sum(jnp.where(tenant_masks[:, :, None], wide, jnp.zeros((), jnp.float32)), axis=1)

    sum_steps = [ring]
    step = ring // 2
    while step >= 1:
        sum_steps.append(step)
        step //= 2

    def sum_step(value, mask):
        sent = hop(value.astype(jnp.bfloat16), [(i, i ^ mask) for i in range(members)])
        return value + sent.astype(jnp.float32)

    own_pieces = [tokens] + [None] * (ring - 1)
    partner_pieces = [None] * ring
    cut = shard_rows // 2
    partner = hop(tokens, swap)
    own_right = hop(tokens, from_right)
    own_left = hop(tokens, from_left)
    partner, own_right, own_left = lax.optimization_barrier((partner, own_right, own_left))
    own_pieces[1], own_pieces[ring - 1] = own_right, own_left
    partner_pieces[0] = partner
    partner_right, partner_left = partner, partner
    low_sum = None
    for step in range(2, ring // 2 + 2):
        moved = []
        if step < ring // 2:
            moved += [hop(own_right, from_right), hop(own_left, from_left)]
        elif step == ring // 2:
            moved += [hop(own_right[:cut], from_right), hop(own_left[cut:], from_left)]
        if step - 1 < ring // 2:
            moved += [hop(partner_right, from_right), hop(partner_left, from_left)]
        else:
            moved += [hop(partner_right[:cut], from_right), hop(partner_left[cut:], from_left)]
        if low_sum is None:
            extra = (local_cols, panels)
        else:
            low_next = sum_step(low_sum, sum_steps.pop(0))
            if step == ring // 2 + 1:
                while sum_steps:
                    low_next = sum_step(low_next, sum_steps.pop(0))
            extra = (low_next,)
        moved, extra = lax.optimization_barrier((moved, extra))
        if low_sum is None:
            local_cols, panels = extra
            down_flat = panels[:, :rank_size, :].reshape(tenants * rank_size, local_width)
            up_flat = panels[:, rank_size:, :].reshape(tenants * rank_size, columns)
            low_sum = partial_of(local_cols)
        else:
            low_sum = extra[0]
        if step < ring // 2:
            own_right, own_left = moved[0], moved[1]
            own_pieces[step], own_pieces[ring - step] = own_right, own_left
            moved = moved[2:]
        elif step == ring // 2:
            own_pieces[step] = jnp.concatenate(moved[:2], axis=0)
            moved = moved[2:]
        if step - 1 < ring // 2:
            partner_right, partner_left = moved
            partner_pieces[step - 1], partner_pieces[ring - step + 1] = partner_right, partner_left
        else:
            partner_pieces[ring // 2] = jnp.concatenate(moved, axis=0)
    for mask in sum_steps:
        low_sum = sum_step(low_sum, mask)

    arrivals = [
        [("own", 0)],
        [("own", 1), ("own", ring - 1), ("partner", 0)],
    ]
    for step in range(2, ring // 2):
        arrivals.append([("own", step), ("own", ring - step), ("partner", step - 1), ("partner", ring - step + 1)])
    arrivals.append([("own", ring // 2), ("partner", ring // 2 - 1), ("partner", ring // 2 + 1)])
    arrivals.append([("partner", ring // 2)])
    pieces = {"own": own_pieces, "partner": partner_pieces}
    base_of = {"own": [None] * ring, "partner": [None] * ring}
    for batch in arrivals:
        stacked = jnp.concatenate([pieces[side][k] for side, k in batch], axis=0)
        product = jnp.dot(stacked, q_weight, preferred_element_type=jnp.float32)
        for i, (side, k) in enumerate(batch):
            base_of[side][k] = product[i * shard_rows:(i + 1) * shard_rows]

    def to_group_order(own_list, partner_list):
        def roll(stacked):
            doubled = jnp.concatenate([stacked, stacked], axis=0)
            return lax.dynamic_slice_in_dim(doubled, (ring - ring_at) % ring, ring, 0)
        own_abs = roll(jnp.stack(own_list))
        partner_abs = roll(jnp.stack(partner_list))
        ordered = jnp.where(
            half == 0, jnp.stack([own_abs, partner_abs]), jnp.stack([partner_abs, own_abs])
        )
        return ordered.reshape((group_rows,) + own_list[0].shape[1:])

    base_projection = to_group_order(base_of["own"], base_of["partner"])
    low_rank = low_sum.astype(jnp.bfloat16)
    low_wide = jnp.where(
        tenant_masks[:, :, None], low_rank[:, None, :], jnp.zeros((), jnp.bfloat16)
    )
    adapter_contribution = jnp.dot(
        low_wide.reshape(group_rows, tenants * rank_size),
        up_flat,
        preferred_element_type=jnp.float32,
    )
    return (base_projection + adapter_scale * adapter_contribution).astype(jnp.bfloat16)


def solution(mesh):
    placed = (
        P(("dp", "tensor"), None),
        P(None, "tensor"),
        P("dp", None, "tensor"),
        P("dp", None, "tensor"),
        P(),
        P(),
        P(),
    )
    return jax.shard_map(
        on_device, mesh=mesh, in_specs=placed, out_specs=P("dp", "tensor"), check_vma=False
    )
```

```python
import jax
import jax.numpy as jnp
from jax import lax
from jax.sharding import PartitionSpec as P

adapter_scale = 0.5


def tenant_mask(pool_unit_row, group_rows, tenants):
    block_ends = 16 * jnp.cumsum(pool_unit_row)
    positions = jnp.arange(group_rows, dtype=jnp.int32)
    tenant_index = jnp.sum((positions[:, None] >= block_ends[None, :]).astype(jnp.int32), axis=1)
    return tenant_index[:, None] == jnp.arange(tenants, dtype=jnp.int32)[None, :]


def tensor_sum(value, members):
    step = 1
    while step < members:
        pairs = [(i, i ^ step) for i in range(members)]
        value = value + lax.ppermute(value, "tensor", pairs)
        step *= 2
    return value


def on_device(tokens, q_weight, pool_down, pool_up, block_units, adapter_ids, location):
    my_group = lax.axis_index("dp")
    groups = adapter_ids.shape[0]
    tenants = adapter_ids.shape[1]
    pool_dev = pool_down.shape[0]
    rank_size = pool_down.shape[1]
    local_width = pool_down.shape[2]
    columns = q_weight.shape[1]

    slot_ids = jnp.take(location, adapter_ids, axis=0)
    slot_shard = slot_ids // pool_dev
    slot_row = slot_ids % pool_dev

    from_me = slot_shard == my_group
    send_row = jnp.sum(jnp.where(from_me, slot_row, 0), axis=1)
    both = jnp.concatenate([pool_down, pool_up], axis=1)
    send = jnp.take(both, send_row, axis=0)
    recv = lax.all_to_all(send, "dp", 0, 0, tiled=True)
    my_src = lax.dynamic_index_in_dim(slot_shard, my_group, 0, keepdims=False)
    panels = jnp.take(recv, my_src, axis=0)

    tensor_at = lax.axis_index("tensor")
    members = lax.axis_size("tensor")
    ring = members // 2
    half = tensor_at // ring
    ring_at = tensor_at % ring
    width_start = tensor_at * local_width
    shard_rows = tokens.shape[0]
    group_rows = shard_rows * members
    pool_unit_row = lax.dynamic_index_in_dim(block_units, my_group, 0, keepdims=False)
    block_ends = 16 * jnp.cumsum(pool_unit_row)

    swap = [(i, i ^ ring) for i in range(members)]
    from_right = [(i, (i // ring) * ring + (i % ring - 1) % ring) for i in range(members)]
    from_left = [(i, (i // ring) * ring + (i % ring + 1) % ring) for i in range(members)]

    def hop(value, pairs):
        return lax.ppermute(value, "tensor", pairs)

    tenant_ids = jnp.arange(tenants, dtype=jnp.int32)
    positions = jnp.arange(group_rows, dtype=jnp.int32)
    tenant_index = jnp.sum((positions[:, None] >= block_ends[None, :]).astype(jnp.int32), axis=1)
    tenant_masks = tenant_index[:, None] == tenant_ids[None, :]

    local_cols = lax.all_to_all(tokens, "tensor", 1, 0, tiled=True)

    def partial_of(cols):
        wide = lax.dot_general(
            cols, down_flat, (((1,), (1,)), ((), ())), preferred_element_type=jnp.float32
        ).reshape(group_rows, tenants, rank_size)
        return jnp.sum(jnp.where(tenant_masks[:, :, None], wide, jnp.zeros((), jnp.float32)), axis=1)

    masks_down = [ring]
    step = ring // 2
    while step >= 1:
        masks_down.append(step)
        step //= 2

    def halve(value, mask):
        upper = (tensor_at & mask) != 0
        cut_at = value.shape[0] // 2
        low_rows, high_rows = value[:cut_at], value[cut_at:]
        kept = jnp.where(upper, high_rows, low_rows)
        sent = jnp.where(upper, low_rows, high_rows)
        return kept + hop(sent, [(i, i ^ mask) for i in range(members)])

    def double(value, mask):
        upper = (tensor_at & mask) != 0
        got = hop(value, [(i, i ^ mask) for i in range(members)])
        return jnp.where(upper, jnp.concatenate([got, value]), jnp.concatenate([value, got]))

    sum_steps = [lambda v, m=m: halve(v, m) for m in masks_down]
    sum_steps.append(lambda v: v.astype(jnp.bfloat16))
    sum_steps += [lambda v, m=m: double(v, m) for m in reversed(masks_down)]
    late_steps = 2

    def sum_step(value, step_fn):
        return step_fn(value)

    own_pieces = [tokens] + [None] * (ring - 1)
    partner_pieces = [None] * ring
    cut = shard_rows // 2
    partner = hop(tokens, swap)
    own_right = hop(tokens, from_right)
    own_left = hop(tokens, from_left)
    partner, own_right, own_left = lax.optimization_barrier((partner, own_right, own_left))
    own_pieces[1], own_pieces[ring - 1] = own_right, own_left
    partner_pieces[0] = partner
    partner_right, partner_left = partner, partner
    low_sum = None
    for step in range(2, ring // 2 + 2):
        moved = []
        if step < ring // 2:
            moved += [hop(own_right, from_right), hop(own_left, from_left)]
        elif step == ring // 2:
            moved += [hop(own_right[:cut], from_right), hop(own_left[cut:], from_left)]
        if step - 1 < ring // 2:
            moved += [hop(partner_right, from_right), hop(partner_left, from_left)]
        else:
            moved += [hop(partner_right[:cut], from_right), hop(partner_left[cut:], from_left)]
        if low_sum is None:
            extra = (local_cols, panels)
        else:
            low_next = sum_step(low_sum, sum_steps.pop(0))
            if step == ring // 2 + 1:
                while len(sum_steps) > late_steps:
                    low_next = sum_step(low_next, sum_steps.pop(0))
            extra = (low_next,)
        moved, extra = lax.optimization_barrier((moved, extra))
        if low_sum is None:
            local_cols, panels = extra
            down_flat = panels[:, :rank_size, :].reshape(tenants * rank_size, local_width)
            up_flat = panels[:, rank_size:, :].reshape(tenants * rank_size, columns)
            low_sum = partial_of(local_cols)
        else:
            low_sum = extra[0]
        if step < ring // 2:
            own_right, own_left = moved[0], moved[1]
            own_pieces[step], own_pieces[ring - step] = own_right, own_left
            moved = moved[2:]
        elif step == ring // 2:
            own_pieces[step] = jnp.concatenate(moved[:2], axis=0)
            moved = moved[2:]
        if step - 1 < ring // 2:
            partner_right, partner_left = moved
            partner_pieces[step - 1], partner_pieces[ring - step + 1] = partner_right, partner_left
        else:
            partner_pieces[ring // 2] = jnp.concatenate(moved, axis=0)
    for mask in sum_steps:
        low_sum = sum_step(low_sum, mask)

    arrivals = [
        [("own", 0)],
        [("own", 1), ("own", ring - 1), ("partner", 0)],
    ]
    for step in range(2, ring // 2):
        arrivals.append([("own", step), ("own", ring - step), ("partner", step - 1), ("partner", ring - step + 1)])
    arrivals.append([("own", ring // 2), ("partner", ring // 2 - 1), ("partner", ring // 2 + 1)])
    arrivals.append([("partner", ring // 2)])
    pieces = {"own": own_pieces, "partner": partner_pieces}
    base_of = {"own": [None] * ring, "partner": [None] * ring}
    for batch in arrivals:
        stacked = jnp.concatenate([pieces[side][k] for side, k in batch], axis=0)
        product = jnp.dot(stacked, q_weight, preferred_element_type=jnp.float32)
        for i, (side, k) in enumerate(batch):
            base_of[side][k] = product[i * shard_rows:(i + 1) * shard_rows]

    def to_group_order(own_list, partner_list):
        def roll(stacked):
            doubled = jnp.concatenate([stacked, stacked], axis=0)
            return lax.dynamic_slice_in_dim(doubled, (ring - ring_at) % ring, ring, 0)
        own_abs = roll(jnp.stack(own_list))
        partner_abs = roll(jnp.stack(partner_list))
        ordered = jnp.where(
            half == 0, jnp.stack([own_abs, partner_abs]), jnp.stack([partner_abs, own_abs])
        )
        return ordered.reshape((group_rows,) + own_list[0].shape[1:])

    base_projection = to_group_order(base_of["own"], base_of["partner"])
    low_rank = low_sum
    low_wide = jnp.where(
        tenant_masks[:, :, None], low_rank[:, None, :], jnp.zeros((), jnp.bfloat16)
    )
    adapter_contribution = jnp.dot(
        low_wide.reshape(group_rows, tenants * rank_size),
        up_flat,
        preferred_element_type=jnp.float32,
    )
    return (base_projection + adapter_scale * adapter_contribution).astype(jnp.bfloat16)


def solution(mesh):
    placed = (
        P(("dp", "tensor"), None),
        P(None, "tensor"),
        P("dp", None, "tensor"),
        P("dp", None, "tensor"),
        P(),
        P(),
        P(),
    )
    return jax.shard_map(
        on_device, mesh=mesh, in_specs=placed, out_specs=P("dp", "tensor"), check_vma=False
    )
```

```python
import jax
import jax.numpy as jnp
from jax import lax
from jax.sharding import PartitionSpec as P

adapter_scale = 0.5


def tenant_mask(pool_unit_row, group_rows, tenants):
    block_ends = 16 * jnp.cumsum(pool_unit_row)
    positions = jnp.arange(group_rows, dtype=jnp.int32)
    tenant_index = jnp.sum((positions[:, None] >= block_ends[None, :]).astype(jnp.int32), axis=1)
    return tenant_index[:, None] == jnp.arange(tenants, dtype=jnp.int32)[None, :]


def tensor_sum(value, members):
    step = 1
    while step < members:
        pairs = [(i, i ^ step) for i in range(members)]
        value = value + lax.ppermute(value, "tensor", pairs)
        step *= 2
    return value


def on_device(tokens, q_weight, pool_down, pool_up, block_units, adapter_ids, location):
    my_group = lax.axis_index("dp")
    groups = adapter_ids.shape[0]
    tenants = adapter_ids.shape[1]
    pool_dev = pool_down.shape[0]
    rank_size = pool_down.shape[1]
    local_width = pool_down.shape[2]
    columns = q_weight.shape[1]

    slot_ids = jnp.take(location, adapter_ids, axis=0)
    slot_shard = slot_ids // pool_dev
    slot_row = slot_ids % pool_dev

    from_me = slot_shard == my_group
    send_row = jnp.sum(jnp.where(from_me, slot_row, 0), axis=1)
    both = jnp.concatenate([pool_down, pool_up], axis=1)
    send = jnp.take(both, send_row, axis=0)
    recv = lax.all_to_all(send, "dp", 0, 0, tiled=True)
    my_src = lax.dynamic_index_in_dim(slot_shard, my_group, 0, keepdims=False)
    panels = jnp.take(recv, my_src, axis=0)

    tensor_at = lax.axis_index("tensor")
    members = lax.axis_size("tensor")
    ring = members // 2
    half = tensor_at // ring
    ring_at = tensor_at % ring
    width_start = tensor_at * local_width
    shard_rows = tokens.shape[0]
    group_rows = shard_rows * members
    pool_unit_row = lax.dynamic_index_in_dim(block_units, my_group, 0, keepdims=False)
    block_ends = 16 * jnp.cumsum(pool_unit_row)

    swap = [(i, i ^ ring) for i in range(members)]
    from_right = [(i, (i // ring) * ring + (i % ring - 1) % ring) for i in range(members)]
    from_left = [(i, (i // ring) * ring + (i % ring + 1) % ring) for i in range(members)]

    def hop(value, pairs):
        return lax.ppermute(value, "tensor", pairs)

    tenant_ids = jnp.arange(tenants, dtype=jnp.int32)
    positions = jnp.arange(group_rows, dtype=jnp.int32)
    tenant_index = jnp.sum((positions[:, None] >= block_ends[None, :]).astype(jnp.int32), axis=1)
    tenant_masks = tenant_index[:, None] == tenant_ids[None, :]

    local_cols = lax.all_to_all(tokens, "tensor", 1, 0, tiled=True)

    def partial_of(cols):
        wide = lax.dot_general(
            cols, down_flat, (((1,), (1,)), ((), ())), preferred_element_type=jnp.float32
        ).reshape(group_rows, tenants, rank_size)
        return jnp.sum(jnp.where(tenant_masks[:, :, None], wide, jnp.zeros((), jnp.float32)), axis=1)

    sum_steps = [ring]
    step = 1
    while step < ring:
        sum_steps.append(step)
        step *= 2

    def sum_step(value, mask):
        return value + hop(value, [(i, i ^ mask) for i in range(members)])

    own_pieces = [tokens] + [None] * (ring - 1)
    partner_pieces = [None] * ring
    cut = shard_rows // 2
    partner = hop(tokens, swap)
    own_right = hop(tokens, from_right)
    own_left = hop(tokens, from_left)
    partner, own_right, own_left = lax.optimization_barrier((partner, own_right, own_left))
    own_pieces[1], own_pieces[ring - 1] = own_right, own_left
    partner_pieces[0] = partner
    partner_right, partner_left = partner, partner
    low_sum = None
    for step in range(2, ring // 2 + 2):
        moved = []
        if step < ring // 2:
            moved += [hop(own_right, from_right), hop(own_left, from_left)]
        elif step == ring // 2:
            moved += [hop(own_right[:cut], from_right), hop(own_left[cut:], from_left)]
        if step - 1 < ring // 2:
            moved += [hop(partner_right, from_right), hop(partner_left, from_left)]
        else:
            moved += [hop(partner_right[:cut], from_right), hop(partner_left[cut:], from_left)]
        if low_sum is None:
            extra = (local_cols, panels)
        else:
            low_next = sum_step(low_sum, sum_steps.pop(0))
            if step == 3:
                low_next = sum_step(low_next, sum_steps.pop(0))
            if step == ring // 2 + 1:
                while sum_steps:
                    low_next = sum_step(low_next, sum_steps.pop(0))
            extra = (low_next,)
        moved, extra = lax.optimization_barrier((moved, extra))
        if low_sum is None:
            local_cols, panels = extra
            down_flat = panels[:, :rank_size, :].reshape(tenants * rank_size, local_width)
            up_flat = panels[:, rank_size:, :].reshape(tenants * rank_size, columns)
            low_sum = partial_of(local_cols)
        else:
            low_sum = extra[0]
        if step < ring // 2:
            own_right, own_left = moved[0], moved[1]
            own_pieces[step], own_pieces[ring - step] = own_right, own_left
            moved = moved[2:]
        elif step == ring // 2:
            own_pieces[step] = jnp.concatenate(moved[:2], axis=0)
            moved = moved[2:]
        if step - 1 < ring // 2:
            partner_right, partner_left = moved
            partner_pieces[step - 1], partner_pieces[ring - step + 1] = partner_right, partner_left
        else:
            partner_pieces[ring // 2] = jnp.concatenate(moved, axis=0)
    for mask in sum_steps:
        low_sum = sum_step(low_sum, mask)

    arrivals = [
        [("own", 0)],
        [("own", 1), ("own", ring - 1), ("partner", 0)],
    ]
    for step in range(2, ring // 2):
        arrivals.append([("own", step), ("own", ring - step), ("partner", step - 1), ("partner", ring - step + 1)])
    arrivals.append([("own", ring // 2), ("partner", ring // 2 - 1), ("partner", ring // 2 + 1)])
    arrivals.append([("partner", ring // 2)])
    pieces = {"own": own_pieces, "partner": partner_pieces}
    base_of = {"own": [None] * ring, "partner": [None] * ring}
    for batch in arrivals:
        stacked = jnp.concatenate([pieces[side][k] for side, k in batch], axis=0)
        product = jnp.dot(stacked, q_weight, preferred_element_type=jnp.float32)
        for i, (side, k) in enumerate(batch):
            base_of[side][k] = product[i * shard_rows:(i + 1) * shard_rows]

    def to_group_order(own_list, partner_list):
        def roll(stacked):
            doubled = jnp.concatenate([stacked, stacked], axis=0)
            return lax.dynamic_slice_in_dim(doubled, (ring - ring_at) % ring, ring, 0)
        own_abs = roll(jnp.stack(own_list))
        partner_abs = roll(jnp.stack(partner_list))
        ordered = jnp.where(
            half == 0, jnp.stack([own_abs, partner_abs]), jnp.stack([partner_abs, own_abs])
        )
        return ordered.reshape((group_rows,) + own_list[0].shape[1:])

    base_projection = to_group_order(base_of["own"], base_of["partner"])
    low_rank = low_sum.astype(jnp.bfloat16)
    low_wide = jnp.where(
        tenant_masks[:, :, None], low_rank[:, None, :], jnp.zeros((), jnp.bfloat16)
    )
    adapter_contribution = jnp.dot(
        low_wide.reshape(group_rows, tenants * rank_size),
        up_flat,
        preferred_element_type=jnp.float32,
    )
    return (base_projection + adapter_scale * adapter_contribution).astype(jnp.bfloat16)


def solution(mesh):
    placed = (
        P(("dp", "tensor"), None),
        P(None, "tensor"),
        P("dp", None, "tensor"),
        P("dp", None, "tensor"),
        P(),
        P(),
        P(),
    )
    return jax.shard_map(
        on_device, mesh=mesh, in_specs=placed, out_specs=P("dp", "tensor"), check_vma=False
    )
```

```python
import jax
import jax.numpy as jnp
from jax import lax
from jax.sharding import PartitionSpec as P

adapter_scale = 0.5


def tenant_mask(pool_unit_row, group_rows, tenants):
    block_ends = 16 * jnp.cumsum(pool_unit_row)
    positions = jnp.arange(group_rows, dtype=jnp.int32)
    tenant_index = jnp.sum((positions[:, None] >= block_ends[None, :]).astype(jnp.int32), axis=1)
    return tenant_index[:, None] == jnp.arange(tenants, dtype=jnp.int32)[None, :]


def tensor_sum(value, members):
    step = 1
    while step < members:
        pairs = [(i, i ^ step) for i in range(members)]
        value = value + lax.ppermute(value, "tensor", pairs)
        step *= 2
    return value


def on_device(tokens, q_weight, pool_down, pool_up, block_units, adapter_ids, location):
    my_group = lax.axis_index("dp")
    groups = adapter_ids.shape[0]
    tenants = adapter_ids.shape[1]
    pool_dev = pool_down.shape[0]
    rank_size = pool_down.shape[1]
    local_width = pool_down.shape[2]
    columns = q_weight.shape[1]

    slot_ids = jnp.take(location, adapter_ids, axis=0)
    slot_shard = slot_ids // pool_dev
    slot_row = slot_ids % pool_dev

    from_me = slot_shard == my_group
    send_row = jnp.sum(jnp.where(from_me, slot_row, 0), axis=1)
    both = jnp.concatenate([pool_down, pool_up], axis=1)
    send = jnp.take(both, send_row, axis=0)
    recv = lax.all_to_all(send, "dp", 0, 0, tiled=True)
    my_src = lax.dynamic_index_in_dim(slot_shard, my_group, 0, keepdims=False)
    panels = jnp.take(recv, my_src, axis=0)

    tensor_at = lax.axis_index("tensor")
    members = lax.axis_size("tensor")
    ring = members // 2
    half = tensor_at // ring
    ring_at = tensor_at % ring
    width_start = tensor_at * local_width
    shard_rows = tokens.shape[0]
    group_rows = shard_rows * members
    pool_unit_row = lax.dynamic_index_in_dim(block_units, my_group, 0, keepdims=False)
    block_ends = 16 * jnp.cumsum(pool_unit_row)

    swap = [(i, i ^ ring) for i in range(members)]
    from_right = [(i, (i // ring) * ring + (i % ring - 1) % ring) for i in range(members)]
    from_left = [(i, (i // ring) * ring + (i % ring + 1) % ring) for i in range(members)]

    def hop(value, pairs):
        return lax.ppermute(value, "tensor", pairs)

    tenant_ids = jnp.arange(tenants, dtype=jnp.int32)
    positions = jnp.arange(group_rows, dtype=jnp.int32)
    tenant_index = jnp.sum((positions[:, None] >= block_ends[None, :]).astype(jnp.int32), axis=1)
    tenant_masks = tenant_index[:, None] == tenant_ids[None, :]

    local_cols = lax.all_to_all(tokens, "tensor", 1, 0, tiled=True)

    def partial_of(cols):
        wide = lax.dot_general(
            cols, down_flat, (((1,), (1,)), ((), ())), preferred_element_type=jnp.float32
        ).reshape(group_rows, tenants, rank_size)
        return jnp.sum(jnp.where(tenant_masks[:, :, None], wide, jnp.zeros((), jnp.float32)), axis=1)

    sum_steps = [ring]
    step = ring // 2
    while step >= 1:
        sum_steps.append(step)
        step //= 2

    back_two = [(i, (i // ring) * ring + (i % ring - 2) % ring) for i in range(members)]

    def sum_step(value, mask):
        if mask != ring // 2:
            return value + hop(value, [(i, i ^ mask) for i in range(members)])
        split = value.shape[0] // 2
        straight = hop(value[:split], [(i, i ^ mask) for i in range(members)])
        around = hop(hop(value[split:], back_two), back_two)
        return value + jnp.concatenate([straight, around], axis=0)

    own_pieces = [tokens] + [None] * (ring - 1)
    partner_pieces = [None] * ring
    cut = shard_rows // 2
    partner = hop(tokens, swap)
    own_right = hop(tokens, from_right)
    own_left = hop(tokens, from_left)
    partner, own_right, own_left = lax.optimization_barrier((partner, own_right, own_left))
    own_pieces[1], own_pieces[ring - 1] = own_right, own_left
    partner_pieces[0] = partner
    partner_right, partner_left = partner, partner
    low_sum = None
    for step in range(2, ring // 2 + 2):
        moved = []
        if step < ring // 2:
            moved += [hop(own_right, from_right), hop(own_left, from_left)]
        elif step == ring // 2:
            moved += [hop(own_right[:cut], from_right), hop(own_left[cut:], from_left)]
        if step - 1 < ring // 2:
            moved += [hop(partner_right, from_right), hop(partner_left, from_left)]
        else:
            moved += [hop(partner_right[:cut], from_right), hop(partner_left[cut:], from_left)]
        if low_sum is None:
            extra = (local_cols, panels)
        else:
            low_next = sum_step(low_sum, sum_steps.pop(0))
            if step == ring // 2 + 1:
                while sum_steps:
                    low_next = sum_step(low_next, sum_steps.pop(0))
            extra = (low_next,)
        moved, extra = lax.optimization_barrier((moved, extra))
        if low_sum is None:
            local_cols, panels = extra
            down_flat = panels[:, :rank_size, :].reshape(tenants * rank_size, local_width)
            up_flat = panels[:, rank_size:, :].reshape(tenants * rank_size, columns)
            low_sum = partial_of(local_cols)
        else:
            low_sum = extra[0]
        if step < ring // 2:
            own_right, own_left = moved[0], moved[1]
            own_pieces[step], own_pieces[ring - step] = own_right, own_left
            moved = moved[2:]
        elif step == ring // 2:
            own_pieces[step] = jnp.concatenate(moved[:2], axis=0)
            moved = moved[2:]
        if step - 1 < ring // 2:
            partner_right, partner_left = moved
            partner_pieces[step - 1], partner_pieces[ring - step + 1] = partner_right, partner_left
        else:
            partner_pieces[ring // 2] = jnp.concatenate(moved, axis=0)
    for mask in sum_steps:
        low_sum = sum_step(low_sum, mask)

    arrivals = [
        [("own", 0)],
        [("own", 1), ("own", ring - 1), ("partner", 0)],
    ]
    for step in range(2, ring // 2):
        arrivals.append([("own", step), ("own", ring - step), ("partner", step - 1), ("partner", ring - step + 1)])
    arrivals.append([("own", ring // 2), ("partner", ring // 2 - 1), ("partner", ring // 2 + 1)])
    arrivals.append([("partner", ring // 2)])
    pieces = {"own": own_pieces, "partner": partner_pieces}
    base_of = {"own": [None] * ring, "partner": [None] * ring}
    for batch in arrivals:
        stacked = jnp.concatenate([pieces[side][k] for side, k in batch], axis=0)
        product = jnp.dot(stacked, q_weight, preferred_element_type=jnp.float32)
        for i, (side, k) in enumerate(batch):
            base_of[side][k] = product[i * shard_rows:(i + 1) * shard_rows]

    def to_group_order(own_list, partner_list):
        def roll(stacked):
            doubled = jnp.concatenate([stacked, stacked], axis=0)
            return lax.dynamic_slice_in_dim(doubled, (ring - ring_at) % ring, ring, 0)
        own_abs = roll(jnp.stack(own_list))
        partner_abs = roll(jnp.stack(partner_list))
        ordered = jnp.where(
            half == 0, jnp.stack([own_abs, partner_abs]), jnp.stack([partner_abs, own_abs])
        )
        return ordered.reshape((group_rows,) + own_list[0].shape[1:])

    base_projection = to_group_order(base_of["own"], base_of["partner"])
    low_rank = low_sum.astype(jnp.bfloat16)
    low_wide = jnp.where(
        tenant_masks[:, :, None], low_rank[:, None, :], jnp.zeros((), jnp.bfloat16)
    )
    adapter_contribution = jnp.dot(
        low_wide.reshape(group_rows, tenants * rank_size),
        up_flat,
        preferred_element_type=jnp.float32,
    )
    return (base_projection + adapter_scale * adapter_contribution).astype(jnp.bfloat16)


def solution(mesh):
    placed = (
        P(("dp", "tensor"), None),
        P(None, "tensor"),
        P("dp", None, "tensor"),
        P("dp", None, "tensor"),
        P(),
        P(),
        P(),
    )
    return jax.shard_map(
        on_device, mesh=mesh, in_specs=placed, out_specs=P("dp", "tensor"), check_vma=False
    )
```

```python
import jax
import jax.numpy as jnp
from jax import lax
from jax.sharding import PartitionSpec as P

adapter_scale = 0.5


def tenant_mask(pool_unit_row, group_rows, tenants):
    block_ends = 16 * jnp.cumsum(pool_unit_row)
    positions = jnp.arange(group_rows, dtype=jnp.int32)
    tenant_index = jnp.sum((positions[:, None] >= block_ends[None, :]).astype(jnp.int32), axis=1)
    return tenant_index[:, None] == jnp.arange(tenants, dtype=jnp.int32)[None, :]


def tensor_sum(value, members):
    step = 1
    while step < members:
        pairs = [(i, i ^ step) for i in range(members)]
        value = value + lax.ppermute(value, "tensor", pairs)
        step *= 2
    return value


def on_device(tokens, q_weight, pool_down, pool_up, block_units, adapter_ids, location):
    my_group = lax.axis_index("dp")
    groups = adapter_ids.shape[0]
    tenants = adapter_ids.shape[1]
    pool_dev = pool_down.shape[0]
    rank_size = pool_down.shape[1]
    local_width = pool_down.shape[2]
    columns = q_weight.shape[1]

    slot_ids = jnp.take(location, adapter_ids, axis=0)
    slot_shard = slot_ids // pool_dev
    slot_row = slot_ids % pool_dev

    from_me = slot_shard == my_group
    send_row = jnp.sum(jnp.where(from_me, slot_row, 0), axis=1)
    both = jnp.concatenate([pool_down, pool_up], axis=1)
    send = jnp.take(both, send_row, axis=0)
    recv = lax.all_to_all(send, "dp", 0, 0, tiled=True)
    my_src = lax.dynamic_index_in_dim(slot_shard, my_group, 0, keepdims=False)
    panels = jnp.take(recv, my_src, axis=0)

    tensor_at = lax.axis_index("tensor")
    members = lax.axis_size("tensor")
    ring = members // 2
    half = tensor_at // ring
    ring_at = tensor_at % ring
    width_start = tensor_at * local_width
    shard_rows = tokens.shape[0]
    group_rows = shard_rows * members
    pool_unit_row = lax.dynamic_index_in_dim(block_units, my_group, 0, keepdims=False)
    block_ends = 16 * jnp.cumsum(pool_unit_row)

    swap = [(i, i ^ ring) for i in range(members)]
    from_right = [(i, (i // ring) * ring + (i % ring - 1) % ring) for i in range(members)]
    from_left = [(i, (i // ring) * ring + (i % ring + 1) % ring) for i in range(members)]

    def hop(value, pairs):
        return lax.ppermute(value, "tensor", pairs)

    tenant_ids = jnp.arange(tenants, dtype=jnp.int32)
    positions = jnp.arange(group_rows, dtype=jnp.int32)
    tenant_index = jnp.sum((positions[:, None] >= block_ends[None, :]).astype(jnp.int32), axis=1)
    tenant_masks = tenant_index[:, None] == tenant_ids[None, :]

    local_cols = lax.all_to_all(tokens, "tensor", 1, 0, tiled=True)

    def partial_of(cols):
        wide = lax.dot_general(
            cols, down_flat, (((1,), (1,)), ((), ())), preferred_element_type=jnp.float32
        ).reshape(group_rows, tenants, rank_size)
        return jnp.sum(jnp.where(tenant_masks[:, :, None], wide, jnp.zeros((), jnp.float32)), axis=1)

    sum_steps = [ring // 2, ring]
    step = ring // 4
    while step >= 1:
        sum_steps.append(step)
        step //= 2

    def sum_step(value, mask):
        return value + hop(value, [(i, i ^ mask) for i in range(members)])

    own_pieces = [tokens] + [None] * (ring - 1)
    partner_pieces = [None] * ring
    cut = shard_rows // 2
    partner = hop(tokens, swap)
    own_right = hop(tokens, from_right)
    own_left = hop(tokens, from_left)
    partner, own_right, own_left = lax.optimization_barrier((partner, own_right, own_left))
    own_pieces[1], own_pieces[ring - 1] = own_right, own_left
    partner_pieces[0] = partner
    partner_right, partner_left = partner, partner
    low_sum = None
    for step in range(2, ring // 2 + 2):
        moved = []
        if step < ring // 2:
            moved += [hop(own_right, from_right), hop(own_left, from_left)]
        elif step == ring // 2:
            moved += [hop(own_right[:cut], from_right), hop(own_left[cut:], from_left)]
        if step - 1 < ring // 2:
            moved += [hop(partner_right, from_right), hop(partner_left, from_left)]
        else:
            moved += [hop(partner_right[:cut], from_right), hop(partner_left[cut:], from_left)]
        if low_sum is None:
            extra = (local_cols, panels)
        else:
            low_next = sum_step(low_sum, sum_steps.pop(0))
            if step == ring // 2 + 1:
                while sum_steps:
                    low_next = sum_step(low_next, sum_steps.pop(0))
            extra = (low_next,)
        moved, extra = lax.optimization_barrier((moved, extra))
        if low_sum is None:
            local_cols, panels = extra
            down_flat = panels[:, :rank_size, :].reshape(tenants * rank_size, local_width)
            up_flat = panels[:, rank_size:, :].reshape(tenants * rank_size, columns)
            low_sum = partial_of(local_cols)
        else:
            low_sum = extra[0]
        if step < ring // 2:
            own_right, own_left = moved[0], moved[1]
            own_pieces[step], own_pieces[ring - step] = own_right, own_left
            moved = moved[2:]
        elif step == ring // 2:
            own_pieces[step] = jnp.concatenate(moved[:2], axis=0)
            moved = moved[2:]
        if step - 1 < ring // 2:
            partner_right, partner_left = moved
            partner_pieces[step - 1], partner_pieces[ring - step + 1] = partner_right, partner_left
        else:
            partner_pieces[ring // 2] = jnp.concatenate(moved, axis=0)
    for mask in sum_steps:
        low_sum = sum_step(low_sum, mask)

    arrivals = [
        [("own", 0)],
        [("own", 1), ("own", ring - 1), ("partner", 0)],
    ]
    for step in range(2, ring // 2):
        arrivals.append([("own", step), ("own", ring - step), ("partner", step - 1), ("partner", ring - step + 1)])
    arrivals.append([("own", ring // 2), ("partner", ring // 2 - 1), ("partner", ring // 2 + 1)])
    arrivals.append([("partner", ring // 2)])
    pieces = {"own": own_pieces, "partner": partner_pieces}
    base_of = {"own": [None] * ring, "partner": [None] * ring}
    for batch in arrivals:
        stacked = jnp.concatenate([pieces[side][k] for side, k in batch], axis=0)
        product = jnp.dot(stacked, q_weight, preferred_element_type=jnp.float32)
        for i, (side, k) in enumerate(batch):
            base_of[side][k] = product[i * shard_rows:(i + 1) * shard_rows]

    def to_group_order(own_list, partner_list):
        def roll(stacked):
            doubled = jnp.concatenate([stacked, stacked], axis=0)
            return lax.dynamic_slice_in_dim(doubled, (ring - ring_at) % ring, ring, 0)
        own_abs = roll(jnp.stack(own_list))
        partner_abs = roll(jnp.stack(partner_list))
        ordered = jnp.where(
            half == 0, jnp.stack([own_abs, partner_abs]), jnp.stack([partner_abs, own_abs])
        )
        return ordered.reshape((group_rows,) + own_list[0].shape[1:])

    base_projection = to_group_order(base_of["own"], base_of["partner"])
    low_rank = low_sum.astype(jnp.bfloat16)
    low_wide = jnp.where(
        tenant_masks[:, :, None], low_rank[:, None, :], jnp.zeros((), jnp.bfloat16)
    )
    adapter_contribution = jnp.dot(
        low_wide.reshape(group_rows, tenants * rank_size),
        up_flat,
        preferred_element_type=jnp.float32,
    )
    return (base_projection + adapter_scale * adapter_contribution).astype(jnp.bfloat16)


def solution(mesh):
    placed = (
        P(("dp", "tensor"), None),
        P(None, "tensor"),
        P("dp", None, "tensor"),
        P("dp", None, "tensor"),
        P(),
        P(),
        P(),
    )
    return jax.shard_map(
        on_device, mesh=mesh, in_specs=placed, out_specs=P("dp", "tensor"), check_vma=False
    )
```

```python
import jax
import jax.numpy as jnp
from jax import lax
from jax.sharding import PartitionSpec as P

adapter_scale = 0.5


def tenant_mask(pool_unit_row, group_rows, tenants):
    block_ends = 16 * jnp.cumsum(pool_unit_row)
    positions = jnp.arange(group_rows, dtype=jnp.int32)
    tenant_index = jnp.sum((positions[:, None] >= block_ends[None, :]).astype(jnp.int32), axis=1)
    return tenant_index[:, None] == jnp.arange(tenants, dtype=jnp.int32)[None, :]


def tensor_sum(value, members):
    step = 1
    while step < members:
        pairs = [(i, i ^ step) for i in range(members)]
        value = value + lax.ppermute(value, "tensor", pairs)
        step *= 2
    return value


def on_device(tokens, q_weight, pool_down, pool_up, block_units, adapter_ids, location):
    my_group = lax.axis_index("dp")
    groups = adapter_ids.shape[0]
    tenants = adapter_ids.shape[1]
    pool_dev = pool_down.shape[0]
    rank_size = pool_down.shape[1]
    local_width = pool_down.shape[2]
    columns = q_weight.shape[1]

    slot_ids = jnp.take(location, adapter_ids, axis=0)
    slot_shard = slot_ids // pool_dev
    slot_row = slot_ids % pool_dev

    from_me = slot_shard == my_group
    send_row = jnp.sum(jnp.where(from_me, slot_row, 0), axis=1)
    both = jnp.concatenate([pool_down, pool_up], axis=1)
    send = jnp.take(both, send_row, axis=0)
    recv = lax.all_to_all(send, "dp", 0, 0, tiled=True)
    my_src = lax.dynamic_index_in_dim(slot_shard, my_group, 0, keepdims=False)
    panels = jnp.take(recv, my_src, axis=0)

    tensor_at = lax.axis_index("tensor")
    members = lax.axis_size("tensor")
    ring = members // 2
    half = tensor_at // ring
    ring_at = tensor_at % ring
    width_start = tensor_at * local_width
    shard_rows = tokens.shape[0]
    group_rows = shard_rows * members
    pool_unit_row = lax.dynamic_index_in_dim(block_units, my_group, 0, keepdims=False)
    block_ends = 16 * jnp.cumsum(pool_unit_row)

    swap = [(i, i ^ ring) for i in range(members)]
    from_right = [(i, (i // ring) * ring + (i % ring - 1) % ring) for i in range(members)]
    from_left = [(i, (i // ring) * ring + (i % ring + 1) % ring) for i in range(members)]

    def hop(value, pairs):
        return lax.ppermute(value, "tensor", pairs)

    tenant_ids = jnp.arange(tenants, dtype=jnp.int32)
    positions = jnp.arange(group_rows, dtype=jnp.int32)
    tenant_index = jnp.sum((positions[:, None] >= block_ends[None, :]).astype(jnp.int32), axis=1)
    tenant_masks = tenant_index[:, None] == tenant_ids[None, :]

    local_cols = lax.all_to_all(tokens, "tensor", 1, 0, tiled=True)

    def partial_of(cols):
        wide = lax.dot_general(
            cols, down_flat, (((1,), (1,)), ((), ())), preferred_element_type=jnp.float32
        ).reshape(group_rows, tenants, rank_size)
        return jnp.sum(jnp.where(tenant_masks[:, :, None], wide, jnp.zeros((), jnp.float32)), axis=1)

    sum_steps = [ring]
    step = ring // 2
    while step >= 1:
        sum_steps.append(step)
        step //= 2

    def sum_step(value, mask):
        return value + hop(value, [(i, i ^ mask) for i in range(members)])

    own_pieces = [tokens] + [None] * (ring - 1)
    partner_pieces = [None] * ring
    cut = shard_rows // 2
    partner = hop(tokens, swap)
    own_right = hop(tokens, from_right)
    own_left = hop(tokens, from_left)
    partner, own_right, own_left = lax.optimization_barrier((partner, own_right, own_left))
    own_pieces[1], own_pieces[ring - 1] = own_right, own_left
    partner_pieces[0] = partner
    partner_right, partner_left = partner, partner
    low_sum = None
    for step in range(2, ring // 2 + 2):
        moved = []
        if step < ring // 2:
            moved += [hop(own_right, from_right), hop(own_left, from_left)]
        elif step == ring // 2:
            moved += [hop(own_right[:cut], from_right), hop(own_left[cut:], from_left)]
        if step - 1 < ring // 2:
            moved += [hop(partner_right, from_right), hop(partner_left, from_left)]
        else:
            moved += [hop(partner_right[:cut], from_right), hop(partner_left[cut:], from_left)]
        if low_sum is None:
            extra = (local_cols, panels)
        else:
            low_next = sum_step(low_sum, sum_steps.pop(0))
            if step == ring // 2 + 1:
                while sum_steps:
                    low_next = sum_step(low_next, sum_steps.pop(0))
            extra = (low_next,)
        moved, extra = lax.optimization_barrier((moved, extra))
        if low_sum is None:
            local_cols, panels = extra
            down_flat = panels[:, :rank_size, :].reshape(tenants * rank_size, local_width)
            up_flat = panels[:, rank_size:, :].reshape(tenants * rank_size, columns)
            low_sum = partial_of(local_cols)
        else:
            low_sum = extra[0]
        if step < ring // 2:
            own_right, own_left = moved[0], moved[1]
            own_pieces[step], own_pieces[ring - step] = own_right, own_left
            moved = moved[2:]
        elif step == ring // 2:
            own_pieces[step] = jnp.concatenate(moved[:2], axis=0)
            moved = moved[2:]
        if step - 1 < ring // 2:
            partner_right, partner_left = moved
            partner_pieces[step - 1], partner_pieces[ring - step + 1] = partner_right, partner_left
        else:
            partner_pieces[ring // 2] = jnp.concatenate(moved, axis=0)
    for mask in sum_steps:
        low_sum = sum_step(low_sum, mask)

    arrivals = [
        [("own", 0)],
        [("own", 1), ("own", ring - 1), ("partner", 0)],
    ]
    for step in range(2, ring // 2):
        arrivals.append([("own", step), ("own", ring - step), ("partner", step - 1), ("partner", ring - step + 1)])
    arrivals.append([("own", ring // 2), ("partner", ring // 2 - 1), ("partner", ring // 2 + 1)])
    arrivals.append([("partner", ring // 2)])
    pieces = {"own": own_pieces, "partner": partner_pieces}
    base_of = {"own": [None] * ring, "partner": [None] * ring}
    for batch in arrivals:
        stacked = jnp.concatenate([pieces[side][k] for side, k in batch], axis=0)
        product = jnp.dot(stacked, q_weight, preferred_element_type=jnp.float32)
        for i, (side, k) in enumerate(batch):
            base_of[side][k] = product[i * shard_rows:(i + 1) * shard_rows]

    def to_group_order(own_list, partner_list):
        def roll(stacked):
            doubled = jnp.concatenate([stacked, stacked], axis=0)
            return lax.dynamic_slice_in_dim(doubled, (ring - ring_at) % ring, ring, 0)
        own_abs = roll(jnp.stack(own_list))
        partner_abs = roll(jnp.stack(partner_list))
        ordered = jnp.where(
            half == 0, jnp.stack([own_abs, partner_abs]), jnp.stack([partner_abs, own_abs])
        )
        return ordered.reshape((group_rows,) + own_list[0].shape[1:])

    base_rel = jnp.stack([jnp.stack(base_of["own"]), jnp.stack(base_of["partner"])])
    base_rel = base_rel.reshape(group_rows, columns)
    sides = jnp.arange(2, dtype=jnp.int32)[:, None, None]
    steps = jnp.arange(ring, dtype=jnp.int32)[None, :, None]
    rows = jnp.arange(shard_rows, dtype=jnp.int32)[None, None, :]
    row_half = jnp.where(sides == 0, half, 1 - half)
    row_of = ((row_half * ring + (ring_at + steps) % ring) * shard_rows + rows).reshape(group_rows)
    low_rank = jnp.take(low_sum.astype(jnp.bfloat16), row_of, axis=0)
    masks_rel = jnp.take(tenant_masks, row_of, axis=0)
    low_wide = jnp.where(masks_rel[:, :, None], low_rank[:, None, :], jnp.zeros((), jnp.bfloat16))
    adapter_contribution = jnp.dot(
        low_wide.reshape(group_rows, tenants * rank_size),
        up_flat,
        preferred_element_type=jnp.float32,
    )
    out_rel = (base_rel + adapter_scale * adapter_contribution).astype(jnp.bfloat16)
    out_rel = out_rel.reshape(2, ring, shard_rows, columns)
    return to_group_order([out_rel[0, k] for k in range(ring)], [out_rel[1, k] for k in range(ring)])


def solution(mesh):
    placed = (
        P(("dp", "tensor"), None),
        P(None, "tensor"),
        P("dp", None, "tensor"),
        P("dp", None, "tensor"),
        P(),
        P(),
        P(),
    )
    return jax.shard_map(
        on_device, mesh=mesh, in_specs=placed, out_specs=P("dp", "tensor"), check_vma=False
    )
```
